32 devices in a mesh: group: 2 (over x), row: 8 (over z, y), col: 2 (over core).
Axes of the slice: x: 2, y: 2, z: 4, core: 2. Of those that a mesh axis runs over, the one named last changes fastest.
Arguments:
- observed: float32 [32, 65536], P('group', ('row', 'col')), parts along dimension 0, may hold values from -50 to 50
- blocks: float32 [32, 160, 128, 128], P(('group', 'row', 'col')), parts along dimension 0, may hold values from -0.25 to 0.25
- block_rows: int32 [32, 160], P(('group', 'row', 'col')), parts along dimension 0, may hold values from 0 to 31
- block_cols: int32 [32, 160], P(('group', 'row', 'col')), parts along dimension 0, may hold values from 0 to 191, as said below
- counts: int32 [32], P(('group', 'row', 'col')), parts along dimension 0, may hold values from 32 to 160, as said below
Outputs:
- solution: float32 [32, 131072], P('group', ('row', 'col')), parts along dimension 0
- search_direction: float32 [32, 131072], P('group', ('row', 'col')), parts along dimension 0
The draws below stay inside these ranges and needn't reach their ends.
There are 2 independent parts, one for each index of `group`. The reference program is written for one: setup_inputs(seed, part) draws one part's arguments, and reference() takes and returns one part's arrays. A program takes and returns all parts, laid end to end along the dimension named above; each array names one. Nothing has to cross between parts.
Inputs may be any that keep to these rules, and one draw needn't show every extreme that they name: block_cols of band 0 are 64 or more, those of the last band under 2 * 64. `counts`: some band has exactly 160 live slots.
All inputs are finite; a program needn't handle non-finite values.
Results may differ from the reference program's by a relative error of at most 0.0003.
Values sent between devices are 32-bit elements; how exact they have to be, the bound alone decides.
No kernel may reach another device: no remote copies, remote signals or barrier semaphores. Data moves between devices by JAX's collectives and lax.ppermute only.
A program may use at most 64 MiB of HBM per device.

```python
import jax
import jax.numpy as jnp
from jax import lax

BLOCK_EDGE = 128
SCENARIOS = 16
ROW_BLOCKS = 32
COL_BLOCKS = 64
ITERATIONS = 2
MAX_SLOTS = 160
DEVICE_BANDS = 16
LINK_ROWS = 65536
OD_COLUMNS = 131072


def draw_observed(key, part):
    ramp = 1.0 + 2.0 * jnp.arange(LINK_ROWS).astype(jnp.float32) / LINK_ROWS
    return jnp.clip(jax.random.normal(key, (SCENARIOS, LINK_ROWS), jnp.float32), -4.0, 4.0) * ramp


def draw_block_cols(key, part):
    band_ids = jnp.arange(DEVICE_BANDS).astype(jnp.int32)[:, None]
    lowest = jnp.where(band_ids == 0, COL_BLOCKS, 0)
    highest = jnp.where(band_ids == DEVICE_BANDS - 1, 2 * COL_BLOCKS, 3 * COL_BLOCKS)
    lowest = jnp.broadcast_to(lowest, (DEVICE_BANDS, MAX_SLOTS))
    highest = jnp.broadcast_to(highest, (DEVICE_BANDS, MAX_SLOTS))
    return jax.random.randint(key, (DEVICE_BANDS, MAX_SLOTS), lowest, highest).astype(jnp.int32)


def draw_counts(key, part):
    base = jax.random.randint(jax.random.fold_in(key, 1), (DEVICE_BANDS,), MAX_SLOTS // 5, MAX_SLOTS // 2 + 1)
    heavy = jax.random.randint(jax.random.fold_in(key, 2), (), 0, DEVICE_BANDS)
    band_ids = jnp.arange(DEVICE_BANDS).astype(jnp.int32)
    return jnp.where(band_ids == heavy, MAX_SLOTS, base).astype(jnp.int32)


def plant(entries, stream_key, smallest, high):
    shape = entries.shape
    spot = [jax.random.randint(jax.random.fold_in(stream_key, axis), (), 0, shape[axis]) for axis in range(len(shape))]
    entries = entries.at[tuple(spot)].set(smallest)
    longest = shape.index(max(shape))
    spot[longest] = (spot[longest] + 1) % shape[longest]
    return entries.at[tuple(spot)].set(high)


def block_levels(stream_key, shape, split, least, top_value):
    def one(position, shards_of):
        steps = jax.random.uniform(jax.random.fold_in(jax.random.fold_in(stream_key, 6), position), (shards_of,), jnp.float32, least / len(split), top_value / len(split))
        return jnp.repeat(jnp.exp(steps), shape[position] // shards_of).reshape((-1,) + (1,) * (len(shape) - position - 1))

    factor_of = one(*split[0])
    for cut in split[1:]:
        factor_of = factor_of * one(*cut)
    return factor_of


def gaussian(stream_key, dims, deviation, limit, cuts=(), dtype=jnp.bfloat16):
    array = deviation * jax.random.normal(stream_key, dims, jnp.float32)
    if cuts:
        array = array * block_levels(stream_key, dims, cuts, -0.22, 0.18)
    return jnp.clip(array, -limit, limit).astype(dtype)


def setup_inputs(seed: int = 0, part: int = 0) -> dict:
    arg_keys = jax.random.split(jax.random.key(seed), 6)
    part_splits = jax.random.split(jax.random.fold_in(arg_keys[5], part), 6)
    observed = draw_observed(jax.random.fold_in(jax.random.fold_in(arg_keys[5], part), 71), part)
    blocks = gaussian(part_splits[1], (DEVICE_BANDS, MAX_SLOTS, BLOCK_EDGE, BLOCK_EDGE), (4 * BLOCK_EDGE) ** -0.5, 0.25, ((0, 16),), jnp.float32)
    block_rows = plant(jax.random.randint(part_splits[2], (DEVICE_BANDS, MAX_SLOTS), 0, ROW_BLOCKS), jax.random.fold_in(part_splits[2], 1), 0, ROW_BLOCKS - 1).astype(jnp.int32)
    block_cols = draw_block_cols(jax.random.fold_in(jax.random.fold_in(arg_keys[5], part), 71), part)
    counts = draw_counts(jax.random.fold_in(jax.random.fold_in(arg_keys[5], part), 71), part)
    return dict(observed=observed, blocks=blocks, block_rows=block_rows, block_cols=block_cols, counts=counts)


PRECISE = lax.Precision.HIGHEST

def slot_masks(counts):
    slots = jnp.arange(MAX_SLOTS).astype(jnp.int32)
    return (slots[None, :] < counts[:, None]).astype(jnp.float32)

def forward_product(vector, blocks, block_rows, block_cols, masks_all):
    band_width = COL_BLOCKS * BLOCK_EDGE
    padded = jnp.pad(vector, ((0, 0), (band_width, band_width)))

    def one_band(packed):
        band_index, tile_stack, rows_idx, cols_idx, live_slot = packed
        window = lax.dynamic_slice_in_dim(padded, band_index * band_width, 3 * band_width, 1)
        pieces = window.reshape(SCENARIOS, 3 * COL_BLOCKS, BLOCK_EDGE)[:, cols_idx, :]
        products = jnp.einsum('skj,kij->ksi', pieces, tile_stack, precision=PRECISE) * live_slot[:, None, None]
        onehot = (rows_idx[:, None] == jnp.arange(ROW_BLOCKS).astype(jnp.int32)[None, :]).astype(jnp.float32)
        summed = jnp.einsum('kr,ksi->sri', onehot, products, precision=PRECISE)
        return summed.reshape(SCENARIOS, ROW_BLOCKS * BLOCK_EDGE)
    band_ids = jnp.arange(DEVICE_BANDS).astype(jnp.int32)
    result = lax.map(one_band, (band_ids, blocks, block_rows, block_cols, masks_all))
    return jnp.moveaxis(result, 0, 1).reshape(SCENARIOS, LINK_ROWS)

def transpose_product(field, blocks, block_rows, block_cols, masks_all):
    band_fields = jnp.moveaxis(field.reshape(SCENARIOS, DEVICE_BANDS, ROW_BLOCKS * BLOCK_EDGE), 1, 0)

    def one_band(packed):
        rows_field, tile_stack, rows_idx, cols_idx, live_slot = packed
        pieces = rows_field.reshape(SCENARIOS, ROW_BLOCKS, BLOCK_EDGE)[:, rows_idx, :]
        products = jnp.einsum('ski,kij->ksj', pieces, tile_stack, precision=PRECISE) * live_slot[:, None, None]
        onehot = (cols_idx[:, None] == jnp.arange(3 * COL_BLOCKS).astype(jnp.int32)[None, :]).astype(jnp.float32)
        summed = jnp.einsum('kc,ksj->scj', onehot, products, precision=PRECISE)
        return summed.reshape(SCENARIOS, 3, COL_BLOCKS * BLOCK_EDGE)
    partials = lax.map(one_band, (band_fields, blocks, block_rows, block_cols, masks_all))
    zero_slab = jnp.zeros_like(partials[:1, :, 0])
    from_below = jnp.concatenate([zero_slab, partials[:-1, :, 2]], 0)
    from_above = jnp.concatenate([partials[1:, :, 0], zero_slab], 0)
    summed = partials[:, :, 1] + from_below + from_above
    return jnp.moveaxis(summed, 0, 1).reshape(SCENARIOS, OD_COLUMNS)

def vec_norms(field):
    return jnp.sqrt(lax.optimization_barrier(jnp.sum(field * field, axis=1)) + 1e-06)

def reference(observed, blocks, block_rows, block_cols, counts):
    masks_all = slot_masks(counts)
    row_norm = vec_norms(observed)
    left_vec = observed / row_norm[:, None]
    right_raw = transpose_product(left_vec, blocks, block_rows, block_cols, masks_all)
    col_norm = vec_norms(right_raw)
    right_vec = right_raw / col_norm[:, None]
    dir_now = right_vec
    solution = jnp.zeros((SCENARIOS, OD_COLUMNS), jnp.float32)
    phi_bar = row_norm
    diag_bar = col_norm
    for iteration in range(ITERATIONS):
        left_raw = forward_product(right_vec, blocks, block_rows, block_cols, masks_all) - col_norm[:, None] * left_vec
        row_norm = vec_norms(left_raw)
        left_vec = left_raw / row_norm[:, None]
        right_raw = transpose_product(left_vec, blocks, block_rows, block_cols, masks_all) - row_norm[:, None] * right_vec
        col_norm = vec_norms(right_raw)
        right_vec = right_raw / col_norm[:, None]
        diag_new = jnp.sqrt(diag_bar * diag_bar + row_norm * row_norm)
        rot_cosine = diag_bar / diag_new
        rot_sine = row_norm / diag_new
        off_diag = rot_sine * col_norm
        diag_bar = -rot_cosine * col_norm
        phi_now = rot_cosine * phi_bar
        phi_bar = rot_sine * phi_bar
        solution = solution + (phi_now / diag_new)[:, None] * dir_now
        dir_now = right_vec - (off_diag / diag_new)[:, None] * dir_now
    return (solution, dir_now)
```

```python
import jax
import jax.numpy as jnp
from jax import lax
from jax.sharding import PartitionSpec as P

ROW_BLOCKS = 32
COL_BLOCKS = 64
ITERATIONS = 2


PRECISE = lax.Precision.HIGHEST


def with_halo(shard, sides, width):
    for axis, dim in sides:
        peers, length = (lax.axis_size(axis), shard.shape[dim])
        up = [(i, (i + 1) % peers) for i in range(peers - 1)]
        down = [(j, i) for i, j in up]
        last = lax.slice_in_dim(shard, length - width, length, axis=dim)
        leading = lax.slice_in_dim(shard, 0, width, axis=dim)
        before = lax.ppermute(last, axis, up)
        after = lax.ppermute(leading, axis, down)
        shard = jnp.concatenate([before, shard, after], axis=dim)
    return shard


def from_behind(shard, axis, by):
    peers = lax.axis_size(axis)
    pairs = [(i, i + by) for i in range(peers) if 0 <= i + by < peers]
    return lax.ppermute(shard, axis, pairs)


def forward_local(window, tile_stack, rows_idx, cols_idx, live_slot):
    scenario_rows = window.shape[0]
    tile_edge = tile_stack.shape[1]
    pieces = window.reshape(scenario_rows, 3 * COL_BLOCKS, tile_edge)[:, cols_idx, :]
    products = (
        jnp.einsum("skj,kij->ksi", pieces, tile_stack, precision=PRECISE) * live_slot[:, None, None]
    )
    onehot = (rows_idx[:, None] == jnp.arange(ROW_BLOCKS)[None, :]).astype(jnp.float32)
    summed = jnp.einsum("kr,ksi->sri", onehot, products, precision=PRECISE)
    return summed.reshape(scenario_rows, ROW_BLOCKS * tile_edge)


def transpose_local(field, tile_stack, rows_idx, cols_idx, live_slot):
    scenario_rows = field.shape[0]
    tile_edge = tile_stack.shape[1]
    pieces = field.reshape(scenario_rows, ROW_BLOCKS, tile_edge)[:, rows_idx, :]
    products = (
        jnp.einsum("ski,kij->ksj", pieces, tile_stack, precision=PRECISE) * live_slot[:, None, None]
    )
    onehot = (cols_idx[:, None] == jnp.arange(3 * COL_BLOCKS)[None, :]).astype(jnp.float32)
    summed = jnp.einsum("kc,ksj->scj", onehot, products, precision=PRECISE)
    return summed.reshape(scenario_rows, 3 * COL_BLOCKS * tile_edge)


def forward_apply(vector, tile_stack, rows_idx, cols_idx, live_slot):
    window = with_halo(vector, ((("row", "col"), 1),), vector.shape[1])
    return forward_local(window, tile_stack, rows_idx, cols_idx, live_slot)


def transpose_apply(field, tile_stack, rows_idx, cols_idx, live_slot):
    partial_sums = transpose_local(field, tile_stack, rows_idx, cols_idx, live_slot)
    band_width = partial_sums.shape[1] // 3
    lower = partial_sums[:, :band_width]
    middle = partial_sums[:, band_width : 2 * band_width]
    upper = partial_sums[:, 2 * band_width :]
    from_below = from_behind(upper, ("row", "col"), 1)
    from_above = from_behind(lower, ("row", "col"), -1)
    result = middle + from_below + from_above
    return result


def all_sum(values, axes):
    peers = 1
    for axis in axes:
        peers *= lax.axis_size(axis)
    if peers & (peers - 1):
        return lax.psum(values, axes)
    shift = 1
    while shift < peers:
        width = 4 if shift * 4 <= peers else 2
        parts = [values]
        for k in range(1, width):
            pairs = [(i, i ^ (k * shift)) for i in range(peers)]
            parts.append(lax.ppermute(values, axes, pairs))
        if width == 4:
            values = (parts[0] + parts[1]) + (parts[2] + parts[3])
        else:
            values = parts[0] + parts[1]
        shift *= width
    return values


def squares(field):
    return jnp.sum(field * field, axis=1)


def per_device(observed, blocks, block_rows, block_cols, counts):
    tile_stack = blocks[0]
    rows_idx = block_rows[0]
    cols_idx = block_cols[0]
    slot_ids = jnp.arange(tile_stack.shape[0])
    live_slot = (slot_ids < counts[0]).astype(jnp.float32)
    axes = ("row", "col")

    def backward(field):
        return transpose_apply(field, tile_stack, rows_idx, cols_idx, live_slot)

    def forward(vector):
        return forward_apply(vector, tile_stack, rows_idx, cols_idx, live_slot)

    start_raw = backward(observed)
    totals = all_sum(jnp.stack([squares(observed), squares(start_raw)]), axes)
    row_norm = jnp.sqrt(totals[0] + 1e-06)
    col_norm = jnp.sqrt(totals[1] / (row_norm * row_norm) + 1e-06)
    scale = row_norm * col_norm
    left_vec = observed / row_norm[:, None]
    right_vec = start_raw / scale[:, None]
    left_prod = forward(start_raw)
    left_raw = left_prod / scale[:, None] - col_norm[:, None] * left_vec
    dir_now = right_vec
    solution = jnp.zeros_like(dir_now)
    phi_bar = row_norm
    diag_bar = col_norm
    for iteration in range(ITERATIONS):
        right_prod = backward(left_raw)
        row_norm = jnp.sqrt(all_sum(squares(left_raw), axes) + 1e-06)
        left_vec = left_raw / row_norm[:, None]
        right_raw = right_prod / row_norm[:, None] - row_norm[:, None] * right_vec
        if iteration + 1 < ITERATIONS:
            left_prod = forward(right_raw)
        col_norm = jnp.sqrt(all_sum(squares(right_raw), axes) + 1e-06)
        right_vec = right_raw / col_norm[:, None]
        if iteration + 1 < ITERATIONS:
            left_raw = left_prod / col_norm[:, None] - col_norm[:, None] * left_vec
        diag_new = jnp.sqrt(diag_bar * diag_bar + row_norm * row_norm)
        rot_cosine = diag_bar / diag_new
        rot_sine = row_norm / diag_new
        off_diag = rot_sine * col_norm
        diag_bar = -rot_cosine * col_norm
        phi_now = rot_cosine * phi_bar
        phi_bar = rot_sine * phi_bar
        solution = solution + (phi_now / diag_new)[:, None] * dir_now
        dir_now = right_vec - (off_diag / diag_new)[:, None] * dir_now
    return (solution, dir_now)


def solution(mesh):
    in_specs = (
        P("group", ("row", "col")),
        P(("group", "row", "col"), None, None, None),
        P(("group", "row", "col"), None),
        P(("group", "row", "col"), None),
        P(("group", "row", "col")),
    )
    out_specs = (P("group", ("row", "col")), P("group", ("row", "col")))
    return jax.shard_map(
        per_device, mesh=mesh, in_specs=in_specs, out_specs=out_specs, check_vma=False
    )
```

```python
import jax
import jax.numpy as jnp
from jax import lax
from jax.sharding import PartitionSpec as P

ROW_BLOCKS = 32
COL_BLOCKS = 64
ITERATIONS = 2


PRECISE = lax.Precision.HIGHEST
PRODUCT_PRECISION = lax.Precision.HIGH


def with_halo(shard, sides, width):
    for axis, dim in sides:
        peers, length = (lax.axis_size(axis), shard.shape[dim])
        up = [(i, (i + 1) % peers) for i in range(peers - 1)]
        down = [(j, i) for i, j in up]
        last = lax.slice_in_dim(shard, length - width, length, axis=dim)
        leading = lax.slice_in_dim(shard, 0, width, axis=dim)
        before = lax.ppermute(last, axis, up)
        after = lax.ppermute(leading, axis, down)
        shard = jnp.concatenate([before, shard, after], axis=dim)
    return shard


def from_behind(shard, axis, by):
    peers = lax.axis_size(axis)
    pairs = [(i, i + by) for i in range(peers) if 0 <= i + by < peers]
    return lax.ppermute(shard, axis, pairs)


def forward_local(window, tile_stack, rows_idx, cols_idx, live_slot):
    scenario_rows = window.shape[0]
    tile_edge = tile_stack.shape[1]
    pieces = window.reshape(scenario_rows, 3 * COL_BLOCKS, tile_edge)[:, cols_idx, :]
    products = (
        jnp.einsum("skj,kij->ksi", pieces, tile_stack, precision=PRODUCT_PRECISION) * live_slot[:, None, None]
    )
    onehot = (rows_idx[:, None] == jnp.arange(ROW_BLOCKS)[None, :]).astype(jnp.float32)
    summed = jnp.einsum("kr,ksi->sri", onehot, products, precision=PRECISE)
    return summed.reshape(scenario_rows, ROW_BLOCKS * tile_edge)


def transpose_local(field, tile_stack, rows_idx, cols_idx, live_slot):
    scenario_rows = field.shape[0]
    tile_edge = tile_stack.shape[1]
    pieces = field.reshape(scenario_rows, ROW_BLOCKS, tile_edge)[:, rows_idx, :]
    products = (
        jnp.einsum("ski,kij->ksj", pieces, tile_stack, precision=PRODUCT_PRECISION) * live_slot[:, None, None]
    )
    onehot = (cols_idx[:, None] == jnp.arange(3 * COL_BLOCKS)[None, :]).astype(jnp.float32)
    summed = jnp.einsum("kc,ksj->scj", onehot, products, precision=PRECISE)
    return summed.reshape(scenario_rows, 3 * COL_BLOCKS * tile_edge)


def forward_apply(vector, tile_stack, rows_idx, cols_idx, live_slot):
    window = with_halo(vector, ((("row", "col"), 1),), vector.shape[1])
    return forward_local(window, tile_stack, rows_idx, cols_idx, live_slot)


def transpose_apply(field, tile_stack, rows_idx, cols_idx, live_slot):
    partial_sums = transpose_local(field, tile_stack, rows_idx, cols_idx, live_slot)
    band_width = partial_sums.shape[1] // 3
    lower = partial_sums[:, :band_width]
    middle = partial_sums[:, band_width : 2 * band_width]
    upper = partial_sums[:, 2 * band_width :]
    from_below = from_behind(upper, ("row", "col"), 1)
    from_above = from_behind(lower, ("row", "col"), -1)
    result = middle + from_below + from_above
    return result


def all_sum(values, axes):
    peers = 1
    for axis in axes:
        peers *= lax.axis_size(axis)
    if peers & (peers - 1):
        return lax.psum(values, axes)
    shift = 1
    while shift < peers:
        width = 4 if shift * 4 <= peers else 2
        parts = [values]
        for k in range(1, width):
            pairs = [(i, i ^ (k * shift)) for i in range(peers)]
            parts.append(lax.ppermute(values, axes, pairs))
        if width == 4:
            values = (parts[0] + parts[1]) + (parts[2] + parts[3])
        else:
            values = parts[0] + parts[1]
        shift *= width
    return values


def squares(field):
    return jnp.sum(field * field, axis=1)


def per_device(observed, blocks, block_rows, block_cols, counts):
    tile_stack = blocks[0]
    rows_idx = block_rows[0]
    cols_idx = block_cols[0]
    slot_ids = jnp.arange(tile_stack.shape[0])
    live_slot = (slot_ids < counts[0]).astype(jnp.float32)
    axes = ("row", "col")

    def backward(field):
        return transpose_apply(field, tile_stack, rows_idx, cols_idx, live_slot)

    def forward(vector):
        return forward_apply(vector, tile_stack, rows_idx, cols_idx, live_slot)

    start_raw = backward(observed)
    totals = all_sum(jnp.stack([squares(observed), squares(start_raw)]), axes)
    row_norm = jnp.sqrt(totals[0] + 1e-06)
    col_norm = jnp.sqrt(totals[1] / (row_norm * row_norm) + 1e-06)
    scale = row_norm * col_norm
    left_vec = observed / row_norm[:, None]
    right_vec = start_raw / scale[:, None]
    left_prod = forward(start_raw)
    left_raw = left_prod / scale[:, None] - col_norm[:, None] * left_vec
    dir_now = right_vec
    solution = jnp.zeros_like(dir_now)
    phi_bar = row_norm
    diag_bar = col_norm
    for iteration in range(ITERATIONS):
        right_prod = backward(left_raw)
        row_norm = jnp.sqrt(all_sum(squares(left_raw), axes) + 1e-06)
        left_vec = left_raw / row_norm[:, None]
        right_raw = right_prod / row_norm[:, None] - row_norm[:, None] * right_vec
        if iteration + 1 < ITERATIONS:
            left_prod = forward(right_raw)
        col_norm = jnp.sqrt(all_sum(squares(right_raw), axes) + 1e-06)
        right_vec = right_raw / col_norm[:, None]
        if iteration + 1 < ITERATIONS:
            left_raw = left_prod / col_norm[:, None] - col_norm[:, None] * left_vec
        diag_new = jnp.sqrt(diag_bar * diag_bar + row_norm * row_norm)
        rot_cosine = diag_bar / diag_new
        rot_sine = row_norm / diag_new
        off_diag = rot_sine * col_norm
        diag_bar = -rot_cosine * col_norm
        phi_now = rot_cosine * phi_bar
        phi_bar = rot_sine * phi_bar
        solution = solution + (phi_now / diag_new)[:, None] * dir_now
        dir_now = right_vec - (off_diag / diag_new)[:, None] * dir_now
    return (solution, dir_now)


def solution(mesh):
    in_specs = (
        P("group", ("row", "col")),
        P(("group", "row", "col"), None, None, None),
        P(("group", "row", "col"), None),
        P(("group", "row", "col"), None),
        P(("group", "row", "col")),
    )
    out_specs = (P("group", ("row", "col")), P("group", ("row", "col")))
    return jax.shard_map(
        per_device, mesh=mesh, in_specs=in_specs, out_specs=out_specs, check_vma=False
    )
```

```python
import jax
import jax.numpy as jnp
from jax import lax
from jax.sharding import PartitionSpec as P

ROW_BLOCKS = 32
COL_BLOCKS = 64
ITERATIONS = 2


PRECISE = lax.Precision.HIGHEST
PRODUCT_PRECISION = lax.Precision.HIGH


def with_halo(shard, sides, width):
    for axis, dim in sides:
        peers, length = (lax.axis_size(axis), shard.shape[dim])
        up = [(i, (i + 1) % peers) for i in range(peers - 1)]
        down = [(j, i) for i, j in up]
        last = lax.slice_in_dim(shard, length - width, length, axis=dim)
        leading = lax.slice_in_dim(shard, 0, width, axis=dim)
        before = lax.ppermute(last, axis, up)
        after = lax.ppermute(leading, axis, down)
        shard = jnp.concatenate([before, shard, after], axis=dim)
    return shard


def from_behind(shard, axis, by):
    peers = lax.axis_size(axis)
    pairs = [(i, i + by) for i in range(peers) if 0 <= i + by < peers]
    return lax.ppermute(shard, axis, pairs)


def forward_local(window, tile_stack, rows_idx, cols_idx, live_slot):
    scenario_rows = window.shape[0]
    tile_edge = tile_stack.shape[1]
    pieces = window.reshape(scenario_rows, 3 * COL_BLOCKS, tile_edge)[:, cols_idx, :]
    products = (
        jnp.einsum("skj,kij->ksi", pieces, tile_stack, precision=PRODUCT_PRECISION) * live_slot[:, None, None]
    )
    onehot = (rows_idx[:, None] == jnp.arange(ROW_BLOCKS)[None, :]).astype(jnp.float32)
    summed = jnp.einsum("kr,ksi->sri", onehot, products, precision=PRECISE)
    return summed.reshape(scenario_rows, ROW_BLOCKS * tile_edge)


def transpose_local(field, tile_stack, rows_idx, cols_idx, live_slot):
    scenario_rows = field.shape[0]
    tile_edge = tile_stack.shape[1]
    pieces = field.reshape(scenario_rows, ROW_BLOCKS, tile_edge)[:, rows_idx, :]
    products = (
        jnp.einsum("ski,kij->ksj", pieces, tile_stack, precision=PRODUCT_PRECISION) * live_slot[:, None, None]
    )
    onehot = (cols_idx[:, None] == jnp.arange(3 * COL_BLOCKS)[None, :]).astype(jnp.float32)
    summed = jnp.einsum("kc,ksj->scj", onehot, products, precision=PRECISE)
    return summed.reshape(scenario_rows, 3 * COL_BLOCKS * tile_edge)


def forward_apply(vector, tile_stack, rows_idx, cols_idx, live_slot):
    window = with_halo(vector, ((("row", "col"), 1),), vector.shape[1])
    return forward_local(window, tile_stack, rows_idx, cols_idx, live_slot)


def transpose_apply(field, tile_stack, rows_idx, cols_idx, live_slot):
    partial_sums = transpose_local(field, tile_stack, rows_idx, cols_idx, live_slot)
    band_width = partial_sums.shape[1] // 3
    lower = partial_sums[:, :band_width]
    middle = partial_sums[:, band_width : 2 * band_width]
    upper = partial_sums[:, 2 * band_width :]
    from_below = from_behind(upper, ("row", "col"), 1)
    from_above = from_behind(lower, ("row", "col"), -1)
    result = middle + from_below + from_above
    return result


def all_sum(values, axes):
    peers = 1
    for axis in axes:
        peers *= lax.axis_size(axis)
    spread = jnp.broadcast_to(values[None], (peers,) + values.shape)
    gathered = lax.all_to_all(spread, axes, 0, 0, tiled=True)
    return jnp.sum(gathered, axis=0)


def squares(field):
    return jnp.sum(field * field, axis=1)


def per_device(observed, blocks, block_rows, block_cols, counts):
    tile_stack = blocks[0]
    rows_idx = block_rows[0]
    cols_idx = block_cols[0]
    slot_ids = jnp.arange(tile_stack.shape[0])
    live_slot = (slot_ids < counts[0]).astype(jnp.float32)
    axes = ("row", "col")

    def backward(field):
        return transpose_apply(field, tile_stack, rows_idx, cols_idx, live_slot)

    def forward(vector):
        return forward_apply(vector, tile_stack, rows_idx, cols_idx, live_slot)

    start_raw = backward(observed)
    totals = all_sum(jnp.stack([squares(observed), squares(start_raw)]), axes)
    row_norm = jnp.sqrt(totals[0] + 1e-06)
    col_norm = jnp.sqrt(totals[1] / (row_norm * row_norm) + 1e-06)
    scale = row_norm * col_norm
    left_vec = observed / row_norm[:, None]
    right_vec = start_raw / scale[:, None]
    left_prod = forward(start_raw)
    left_raw = left_prod / scale[:, None] - col_norm[:, None] * left_vec
    dir_now = right_vec
    solution = jnp.zeros_like(dir_now)
    phi_bar = row_norm
    diag_bar = col_norm
    for iteration in range(ITERATIONS):
        right_prod = backward(left_raw)
        row_norm = jnp.sqrt(all_sum(squares(left_raw), axes) + 1e-06)
        left_vec = left_raw / row_norm[:, None]
        right_raw = right_prod / row_norm[:, None] - row_norm[:, None] * right_vec
        if iteration + 1 < ITERATIONS:
            left_prod = forward(right_raw)
        col_norm = jnp.sqrt(all_sum(squares(right_raw), axes) + 1e-06)
        right_vec = right_raw / col_norm[:, None]
        if iteration + 1 < ITERATIONS:
            left_raw = left_prod / col_norm[:, None] - col_norm[:, None] * left_vec
        diag_new = jnp.sqrt(diag_bar * diag_bar + row_norm * row_norm)
        rot_cosine = diag_bar / diag_new
        rot_sine = row_norm / diag_new
        off_diag = rot_sine * col_norm
        diag_bar = -rot_cosine * col_norm
        phi_now = rot_cosine * phi_bar
        phi_bar = rot_sine * phi_bar
        solution = solution + (phi_now / diag_new)[:, None] * dir_now
        dir_now = right_vec - (off_diag / diag_new)[:, None] * dir_now
    return (solution, dir_now)


def solution(mesh):
    in_specs = (
        P("group", ("row", "col")),
        P(("group", "row", "col"), None, None, None),
        P(("group", "row", "col"), None),
        P(("group", "row", "col"), None),
        P(("group", "row", "col")),
    )
    out_specs = (P("group", ("row", "col")), P("group", ("row", "col")))
    return jax.shard_map(
        per_device, mesh=mesh, in_specs=in_specs, out_specs=out_specs, check_vma=False
    )
```

```python
import jax
import jax.numpy as jnp
from jax import lax
from jax.sharding import PartitionSpec as P

ROW_BLOCKS = 32
COL_BLOCKS = 64
ITERATIONS = 2


PRECISE = lax.Precision.HIGHEST
PRODUCT_PRECISION = lax.Precision.HIGH


def with_halo(shard, sides, width):
    for axis, dim in sides:
        peers, length = (lax.axis_size(axis), shard.shape[dim])
        up = [(i, (i + 1) % peers) for i in range(peers - 1)]
        down = [(j, i) for i, j in up]
        last = lax.slice_in_dim(shard, length - width, length, axis=dim)
        leading = lax.slice_in_dim(shard, 0, width, axis=dim)
        before = lax.ppermute(last, axis, up)
        after = lax.ppermute(leading, axis, down)
        shard = jnp.concatenate([before, shard, after], axis=dim)
    return shard


def from_behind(shard, axis, by):
    peers = lax.axis_size(axis)
    pairs = [(i, i + by) for i in range(peers) if 0 <= i + by < peers]
    return lax.ppermute(shard, axis, pairs)


def forward_local(window, tile_stack, rows_idx, cols_idx, live_slot):
    scenario_rows = window.shape[0]
    tile_edge = tile_stack.shape[1]
    pieces = window.reshape(scenario_rows, 3 * COL_BLOCKS, tile_edge)[:, cols_idx, :]
    products = (
        jnp.einsum("skj,kji->ksi", pieces, tile_stack, precision=PRODUCT_PRECISION) * live_slot[:, None, None]
    )
    onehot = (rows_idx[:, None] == jnp.arange(ROW_BLOCKS)[None, :]).astype(jnp.float32)
    summed = jnp.einsum("kr,ksi->sri", onehot, products, precision=PRECISE)
    return summed.reshape(scenario_rows, ROW_BLOCKS * tile_edge)


def transpose_local(field, tile_stack, rows_idx, cols_idx, live_slot):
    scenario_rows = field.shape[0]
    tile_edge = tile_stack.shape[1]
    pieces = field.reshape(scenario_rows, ROW_BLOCKS, tile_edge)[:, rows_idx, :]
    products = (
        jnp.einsum("ski,kij->ksj", pieces, tile_stack, precision=PRODUCT_PRECISION) * live_slot[:, None, None]
    )
    onehot = (cols_idx[:, None] == jnp.arange(3 * COL_BLOCKS)[None, :]).astype(jnp.float32)
    summed = jnp.einsum("kc,ksj->scj", onehot, products, precision=PRECISE)
    return summed.reshape(scenario_rows, 3 * COL_BLOCKS * tile_edge)


def forward_apply(vector, tile_stack, rows_idx, cols_idx, live_slot):
    window = with_halo(vector, ((("row", "col"), 1),), vector.shape[1])
    return forward_local(window, tile_stack, rows_idx, cols_idx, live_slot)


def transpose_apply(field, tile_stack, rows_idx, cols_idx, live_slot):
    partial_sums = transpose_local(field, tile_stack, rows_idx, cols_idx, live_slot)
    band_width = partial_sums.shape[1] // 3
    lower = partial_sums[:, :band_width]
    middle = partial_sums[:, band_width : 2 * band_width]
    upper = partial_sums[:, 2 * band_width :]
    from_below = from_behind(upper, ("row", "col"), 1)
    from_above = from_behind(lower, ("row", "col"), -1)
    result = middle + from_below + from_above
    return result


def all_sum(values, axes):
    peers = 1
    for axis in axes:
        peers *= lax.axis_size(axis)
    spread = jnp.broadcast_to(values[None], (peers,) + values.shape)
    gathered = lax.all_to_all(spread, axes, 0, 0, tiled=True)
    return jnp.sum(gathered, axis=0)


def squares(field):
    return jnp.sum(field * field, axis=1)


def per_device(observed, blocks, block_rows, block_cols, counts):
    tile_stack = blocks[0]
    rows_idx = block_rows[0]
    cols_idx = block_cols[0]
    slot_ids = jnp.arange(tile_stack.shape[0])
    live_slot = (slot_ids < counts[0]).astype(jnp.float32)
    axes = ("row", "col")

    def backward(field):
        return transpose_apply(field, tile_stack, rows_idx, cols_idx, live_slot)

    tile_stack_t = lax.optimization_barrier(jnp.swapaxes(tile_stack, 1, 2))

    def forward(vector):
        return forward_apply(vector, tile_stack_t, rows_idx, cols_idx, live_slot)

    start_raw = backward(observed)
    totals = all_sum(jnp.stack([squares(observed), squares(start_raw)]), axes)
    row_norm = jnp.sqrt(totals[0] + 1e-06)
    col_norm = jnp.sqrt(totals[1] / (row_norm * row_norm) + 1e-06)
    scale = row_norm * col_norm
    left_vec = observed / row_norm[:, None]
    right_vec = start_raw / scale[:, None]
    left_prod = forward(start_raw)
    left_raw = left_prod / scale[:, None] - col_norm[:, None] * left_vec
    dir_now = right_vec
    solution = jnp.zeros_like(dir_now)
    phi_bar = row_norm
    diag_bar = col_norm
    for iteration in range(ITERATIONS):
        right_prod = backward(left_raw)
        row_norm = jnp.sqrt(all_sum(squares(left_raw), axes) + 1e-06)
        left_vec = left_raw / row_norm[:, None]
        right_raw = right_prod / row_norm[:, None] - row_norm[:, None] * right_vec
        if iteration + 1 < ITERATIONS:
            left_prod = forward(right_raw)
        col_norm = jnp.sqrt(all_sum(squares(right_raw), axes) + 1e-06)
        right_vec = right_raw / col_norm[:, None]
        if iteration + 1 < ITERATIONS:
            left_raw = left_prod / col_norm[:, None] - col_norm[:, None] * left_vec
        diag_new = jnp.sqrt(diag_bar * diag_bar + row_norm * row_norm)
        rot_cosine = diag_bar / diag_new
        rot_sine = row_norm / diag_new
        off_diag = rot_sine * col_norm
        diag_bar = -rot_cosine * col_norm
        phi_now = rot_cosine * phi_bar
        phi_bar = rot_sine * phi_bar
        solution = solution + (phi_now / diag_new)[:, None] * dir_now
        dir_now = right_vec - (off_diag / diag_new)[:, None] * dir_now
    return (solution, dir_now)


def solution(mesh):
    in_specs = (
        P("group", ("row", "col")),
        P(("group", "row", "col"), None, None, None),
        P(("group", "row", "col"), None),
        P(("group", "row", "col"), None),
        P(("group", "row", "col")),
    )
    out_specs = (P("group", ("row", "col")), P("group", ("row", "col")))
    return jax.shard_map(
        per_device, mesh=mesh, in_specs=in_specs, out_specs=out_specs, check_vma=False
    )
```

```python
import jax
import jax.numpy as jnp
from jax import lax
from jax.sharding import PartitionSpec as P
from jax.experimental import pallas as pl
from jax.experimental.pallas import tpu as pltpu

ROW_BLOCKS = 32
COL_BLOCKS = 64
ITERATIONS = 2


PRECISE = lax.Precision.HIGHEST
PRODUCT_PRECISION = lax.Precision.HIGH


def with_halo(shard, sides, width):
    for axis, dim in sides:
        peers, length = (lax.axis_size(axis), shard.shape[dim])
        up = [(i, (i + 1) % peers) for i in range(peers - 1)]
        down = [(j, i) for i, j in up]
        last = lax.slice_in_dim(shard, length - width, length, axis=dim)
        leading = lax.slice_in_dim(shard, 0, width, axis=dim)
        before = lax.ppermute(last, axis, up)
        after = lax.ppermute(leading, axis, down)
        shard = jnp.concatenate([before, shard, after], axis=dim)
    return shard


def from_behind(shard, axis, by):
    peers = lax.axis_size(axis)
    pairs = [(i, i + by) for i in range(peers) if 0 <= i + by < peers]
    return lax.ppermute(shard, axis, pairs)


def transpose_blocks(tile_stack):
    slots, edge, _ = tile_stack.shape
    step = 16 if slots % 16 == 0 else 1

    def body(x_ref, o_ref):
        for i in range(step):
            o_ref[i] = x_ref[i].T

    nbytes = 2 * tile_stack.size * tile_stack.dtype.itemsize
    return pl.pallas_call(
        body,
        grid=(slots // step,),
        in_specs=[pl.BlockSpec((step, edge, edge), lambda k: (k, 0, 0))],
        out_specs=pl.BlockSpec((step, edge, edge), lambda k: (k, 0, 0)),
        out_shape=jax.ShapeDtypeStruct(tile_stack.shape, tile_stack.dtype),
        cost_estimate=pl.CostEstimate(flops=0, transcendentals=0, bytes_accessed=nbytes),
    )(tile_stack)


def forward_local(window, tile_stack, rows_idx, cols_idx, live_slot):
    scenario_rows = window.shape[0]
    tile_edge = tile_stack.shape[1]
    pieces = window.reshape(scenario_rows, 3 * COL_BLOCKS, tile_edge)[:, cols_idx, :]
    products = (
        jnp.einsum("skj,kji->ksi", pieces, tile_stack, precision=PRODUCT_PRECISION) * live_slot[:, None, None]
    )
    onehot = (rows_idx[:, None] == jnp.arange(ROW_BLOCKS)[None, :]).astype(jnp.float32)
    summed = jnp.einsum("kr,ksi->sri", onehot, products, precision=PRECISE)
    return summed.reshape(scenario_rows, ROW_BLOCKS * tile_edge)


def transpose_local(field, tile_stack, rows_idx, cols_idx, live_slot):
    scenario_rows = field.shape[0]
    tile_edge = tile_stack.shape[1]
    pieces = field.reshape(scenario_rows, ROW_BLOCKS, tile_edge)[:, rows_idx, :]
    products = (
        jnp.einsum("ski,kij->ksj", pieces, tile_stack, precision=PRODUCT_PRECISION) * live_slot[:, None, None]
    )
    onehot = (cols_idx[:, None] == jnp.arange(3 * COL_BLOCKS)[None, :]).astype(jnp.float32)
    summed = jnp.einsum("kc,ksj->scj", onehot, products, precision=PRECISE)
    return summed.reshape(scenario_rows, 3 * COL_BLOCKS * tile_edge)


def forward_apply(vector, tile_stack, rows_idx, cols_idx, live_slot):
    window = with_halo(vector, ((("row", "col"), 1),), vector.shape[1])
    return forward_local(window, tile_stack, rows_idx, cols_idx, live_slot)


def transpose_apply(field, tile_stack, rows_idx, cols_idx, live_slot):
    partial_sums = transpose_local(field, tile_stack, rows_idx, cols_idx, live_slot)
    band_width = partial_sums.shape[1] // 3
    lower = partial_sums[:, :band_width]
    middle = partial_sums[:, band_width : 2 * band_width]
    upper = partial_sums[:, 2 * band_width :]
    from_below = from_behind(upper, ("row", "col"), 1)
    from_above = from_behind(lower, ("row", "col"), -1)
    result = middle + from_below + from_above
    return result


def all_sum(values, axes):
    peers = 1
    for axis in axes:
        peers *= lax.axis_size(axis)
    spread = jnp.broadcast_to(values[None], (peers,) + values.shape)
    gathered = lax.all_to_all(spread, axes, 0, 0, tiled=True)
    return jnp.sum(gathered, axis=0)


def squares(field):
    return jnp.sum(field * field, axis=1)


def per_device(observed, blocks, block_rows, block_cols, counts):
    tile_stack = blocks[0]
    rows_idx = block_rows[0]
    cols_idx = block_cols[0]
    slot_ids = jnp.arange(tile_stack.shape[0])
    live_slot = (slot_ids < counts[0]).astype(jnp.float32)
    axes = ("row", "col")

    def backward(field):
        return transpose_apply(field, tile_stack, rows_idx, cols_idx, live_slot)

    tile_stack_t = transpose_blocks(tile_stack)

    def forward(vector):
        return forward_apply(vector, tile_stack_t, rows_idx, cols_idx, live_slot)

    start_raw = backward(observed)
    totals = all_sum(jnp.stack([squares(observed), squares(start_raw)]), axes)
    row_norm = jnp.sqrt(totals[0] + 1e-06)
    col_norm = jnp.sqrt(totals[1] / (row_norm * row_norm) + 1e-06)
    scale = row_norm * col_norm
    left_vec = observed / row_norm[:, None]
    right_vec = start_raw / scale[:, None]
    left_prod = forward(start_raw)
    left_raw = left_prod / scale[:, None] - col_norm[:, None] * left_vec
    dir_now = right_vec
    solution = jnp.zeros_like(dir_now)
    phi_bar = row_norm
    diag_bar = col_norm
    for iteration in range(ITERATIONS):
        right_prod = backward(left_raw)
        row_norm = jnp.sqrt(all_sum(squares(left_raw), axes) + 1e-06)
        left_vec = left_raw / row_norm[:, None]
        right_raw = right_prod / row_norm[:, None] - row_norm[:, None] * right_vec
        if iteration + 1 < ITERATIONS:
            left_prod = forward(right_raw)
        col_norm = jnp.sqrt(all_sum(squares(right_raw), axes) + 1e-06)
        right_vec = right_raw / col_norm[:, None]
        if iteration + 1 < ITERATIONS:
            left_raw = left_prod / col_norm[:, None] - col_norm[:, None] * left_vec
        diag_new = jnp.sqrt(diag_bar * diag_bar + row_norm * row_norm)
        rot_cosine = diag_bar / diag_new
        rot_sine = row_norm / diag_new
        off_diag = rot_sine * col_norm
        diag_bar = -rot_cosine * col_norm
        phi_now = rot_cosine * phi_bar
        phi_bar = rot_sine * phi_bar
        solution = solution + (phi_now / diag_new)[:, None] * dir_now
        dir_now = right_vec - (off_diag / diag_new)[:, None] * dir_now
    return (solution, dir_now)


def solution(mesh):
    in_specs = (
        P("group", ("row", "col")),
        P(("group", "row", "col"), None, None, None),
        P(("group", "row", "col"), None),
        P(("group", "row", "col"), None),
        P(("group", "row", "col")),
    )
    out_specs = (P("group", ("row", "col")), P("group", ("row", "col")))
    return jax.shard_map(
        per_device, mesh=mesh, in_specs=in_specs, out_specs=out_specs, check_vma=False
    )
```

```python
import jax
import jax.numpy as jnp
from jax import lax
from jax.sharding import PartitionSpec as P

ROW_BLOCKS = 32
COL_BLOCKS = 64
ITERATIONS = 2


PRECISE = lax.Precision.HIGHEST
PRODUCT_PRECISION = lax.Precision.HIGH


def with_halo(shard, sides, width):
    for axis, dim in sides:
        peers, length = (lax.axis_size(axis), shard.shape[dim])
        up = [(i, (i + 1) % peers) for i in range(peers - 1)]
        down = [(j, i) for i, j in up]
        last = lax.slice_in_dim(shard, length - width, length, axis=dim)
        leading = lax.slice_in_dim(shard, 0, width, axis=dim)
        before = lax.ppermute(last, axis, up)
        after = lax.ppermute(leading, axis, down)
        shard = jnp.concatenate([before, shard, after], axis=dim)
    return shard


def from_behind(shard, axis, by):
    peers = lax.axis_size(axis)
    pairs = [(i, i + by) for i in range(peers) if 0 <= i + by < peers]
    return lax.ppermute(shard, axis, pairs)


def forward_local(window, tile_stack, rows_idx, cols_idx, live_slot):
    scenario_rows = window.shape[0]
    tile_edge = tile_stack.shape[1]
    pieces = window.reshape(scenario_rows, 3 * COL_BLOCKS, tile_edge)[:, cols_idx, :]
    products = (
        jnp.einsum("skj,kij->ksi", pieces, tile_stack, precision=PRODUCT_PRECISION) * live_slot[:, None, None]
    )
    onehot = (rows_idx[:, None] == jnp.arange(ROW_BLOCKS)[None, :]).astype(jnp.float32)
    summed = jnp.einsum("kr,ksi->sri", onehot, products, precision=PRECISE)
    return summed.reshape(scenario_rows, ROW_BLOCKS * tile_edge)


def transpose_local(field, tile_stack, rows_idx, cols_idx, live_slot):
    scenario_rows = field.shape[0]
    tile_edge = tile_stack.shape[1]
    pieces = field.reshape(scenario_rows, ROW_BLOCKS, tile_edge)[:, rows_idx, :]
    products = (
        jnp.einsum("ski,kij->ksj", pieces, tile_stack, precision=PRODUCT_PRECISION) * live_slot[:, None, None]
    )
    onehot = (cols_idx[:, None] == jnp.arange(3 * COL_BLOCKS)[None, :]).astype(jnp.float32)
    summed = jnp.einsum("kc,ksj->scj", onehot, products, precision=PRECISE)
    return summed.reshape(scenario_rows, 3 * COL_BLOCKS * tile_edge)


def forward_apply(vector, tile_stack, rows_idx, cols_idx, live_slot):
    window = with_halo(vector, ((("row", "col"), 1),), vector.shape[1])
    return forward_local(window, tile_stack, rows_idx, cols_idx, live_slot)


def transpose_apply(field, tile_stack, rows_idx, cols_idx, live_slot):
    partial_sums = transpose_local(field, tile_stack, rows_idx, cols_idx, live_slot)
    band_width = partial_sums.shape[1] // 3
    lower = partial_sums[:, :band_width]
    middle = partial_sums[:, band_width : 2 * band_width]
    upper = partial_sums[:, 2 * band_width :]
    from_below = from_behind(upper, ("row", "col"), 1)
    from_above = from_behind(lower, ("row", "col"), -1)
    result = middle + from_below + from_above
    return result


def all_sum(values, axes):
    peers = 1
    for axis in axes:
        peers *= lax.axis_size(axis)
    spread = jnp.broadcast_to(values[None], (peers,) + values.shape)
    gathered = lax.all_to_all(spread, axes, 0, 0, tiled=True)
    return jnp.sum(gathered, axis=0)


def squares(field):
    return jnp.sum(field * field, axis=1)


def per_device(observed, blocks, block_rows, block_cols, counts):
    tile_stack = blocks[0]
    rows_idx = block_rows[0]
    cols_idx = block_cols[0]
    slot_ids = jnp.arange(tile_stack.shape[0])
    live_slot = (slot_ids < counts[0]).astype(jnp.float32)
    axes = ("row", "col")

    def backward(field):
        return transpose_apply(field, tile_stack, rows_idx, cols_idx, live_slot)

    def forward(vector):
        return forward_apply(vector, tile_stack, rows_idx, cols_idx, live_slot)

    start_raw = backward(observed)
    totals = all_sum(jnp.stack([squares(observed), squares(start_raw)]), axes)
    row_norm = jnp.sqrt(totals[0] + 1e-06)
    col_norm = jnp.sqrt(totals[1] / (row_norm * row_norm) + 1e-06)
    scale = row_norm * col_norm
    left_vec = observed / row_norm[:, None]
    right_vec = start_raw / scale[:, None]
    left_prod = forward(start_raw)
    left_raw = left_prod / scale[:, None] - col_norm[:, None] * left_vec
    dir_now = right_vec
    solution = jnp.zeros_like(dir_now)
    phi_bar = row_norm
    diag_bar = col_norm
    for iteration in range(ITERATIONS):
        right_prod = backward(left_raw)
        sums = all_sum(
            jnp.stack(
                [
                    squares(left_raw),
                    squares(right_prod),
                    jnp.sum(right_prod * right_vec, axis=1),
                    squares(right_vec),
                ]
            ),
            axes,
        )
        row_square = sums[0] + 1e-06
        row_norm = jnp.sqrt(row_square)
        left_vec = left_raw / row_norm[:, None]
        right_raw = right_prod / row_norm[:, None] - row_norm[:, None] * right_vec
        if iteration + 1 < ITERATIONS:
            left_prod = forward(right_raw)
        col_square = sums[1] / row_square - 2.0 * sums[2] + row_square * sums[3]
        col_norm = jnp.sqrt(jnp.maximum(col_square, 0.0) + 1e-06)
        right_vec = right_raw / col_norm[:, None]
        if iteration + 1 < ITERATIONS:
            left_raw = left_prod / col_norm[:, None] - col_norm[:, None] * left_vec
        diag_new = jnp.sqrt(diag_bar * diag_bar + row_norm * row_norm)
        rot_cosine = diag_bar / diag_new
        rot_sine = row_norm / diag_new
        off_diag = rot_sine * col_norm
        diag_bar = -rot_cosine * col_norm
        phi_now = rot_cosine * phi_bar
        phi_bar = rot_sine * phi_bar
        solution = solution + (phi_now / diag_new)[:, None] * dir_now
        dir_now = right_vec - (off_diag / diag_new)[:, None] * dir_now
    return (solution, dir_now)


def solution(mesh):
    in_specs = (
        P("group", ("row", "col")),
        P(("group", "row", "col"), None, None, None),
        P(("group", "row", "col"), None),
        P(("group", "row", "col"), None),
        P(("group", "row", "col")),
    )
    out_specs = (P("group", ("row", "col")), P("group", ("row", "col")))
    return jax.shard_map(
        per_device, mesh=mesh, in_specs=in_specs, out_specs=out_specs, check_vma=False
    )
```

```python
import jax
import jax.numpy as jnp
from jax import lax
from jax.sharding import PartitionSpec as P

ROW_BLOCKS = 32
COL_BLOCKS = 64
ITERATIONS = 2


PRECISE = lax.Precision.HIGHEST
PRODUCT_PRECISION = lax.Precision.HIGH


def with_halo(shard, sides, width):
    for axis, dim in sides:
        peers, length = (lax.axis_size(axis), shard.shape[dim])
        up = [(i, (i + 1) % peers) for i in range(peers - 1)]
        down = [(j, i) for i, j in up]
        last = lax.slice_in_dim(shard, length - width, length, axis=dim)
        leading = lax.slice_in_dim(shard, 0, width, axis=dim)
        before = lax.ppermute(last, axis, up)
        after = lax.ppermute(leading, axis, down)
        shard = jnp.concatenate([before, shard, after], axis=dim)
    return shard


def from_behind(shard, axis, by):
    peers = lax.axis_size(axis)
    pairs = [(i, i + by) for i in range(peers) if 0 <= i + by < peers]
    return lax.ppermute(shard, axis, pairs)


def forward_local(window, tile_stack, rows_idx, cols_idx, live_slot):
    scenario_rows = window.shape[0]
    tile_edge = tile_stack.shape[1]
    pieces = window.reshape(scenario_rows, 3 * COL_BLOCKS, tile_edge)[:, cols_idx, :]
    products = (
        jnp.einsum("skj,kij->ksi", pieces, tile_stack, precision=PRODUCT_PRECISION) * live_slot[:, None, None]
    )
    onehot = (rows_idx[:, None] == jnp.arange(ROW_BLOCKS)[None, :]).astype(jnp.float32)
    summed = jnp.einsum("kr,ksi->sri", onehot, products, precision=PRODUCT_PRECISION)
    return summed.reshape(scenario_rows, ROW_BLOCKS * tile_edge)


def transpose_local(field, tile_stack, rows_idx, cols_idx, live_slot):
    scenario_rows = field.shape[0]
    tile_edge = tile_stack.shape[1]
    pieces = field.reshape(scenario_rows, ROW_BLOCKS, tile_edge)[:, rows_idx, :]
    products = (
        jnp.einsum("ski,kij->ksj", pieces, tile_stack, precision=PRODUCT_PRECISION) * live_slot[:, None, None]
    )
    onehot = (cols_idx[:, None] == jnp.arange(3 * COL_BLOCKS)[None, :]).astype(jnp.float32)
    summed = jnp.einsum("kc,ksj->scj", onehot, products, precision=PRODUCT_PRECISION)
    return summed.reshape(scenario_rows, 3 * COL_BLOCKS * tile_edge)


def forward_apply(vector, tile_stack, rows_idx, cols_idx, live_slot):
    window = with_halo(vector, ((("row", "col"), 1),), vector.shape[1])
    return forward_local(window, tile_stack, rows_idx, cols_idx, live_slot)


def transpose_apply(field, tile_stack, rows_idx, cols_idx, live_slot):
    partial_sums = transpose_local(field, tile_stack, rows_idx, cols_idx, live_slot)
    band_width = partial_sums.shape[1] // 3
    lower = partial_sums[:, :band_width]
    middle = partial_sums[:, band_width : 2 * band_width]
    upper = partial_sums[:, 2 * band_width :]
    from_below = from_behind(upper, ("row", "col"), 1)
    from_above = from_behind(lower, ("row", "col"), -1)
    result = middle + from_below + from_above
    return result


def all_sum(values, axes):
    peers = 1
    for axis in axes:
        peers *= lax.axis_size(axis)
    spread = jnp.broadcast_to(values[None], (peers,) + values.shape)
    gathered = lax.all_to_all(spread, axes, 0, 0, tiled=True)
    return jnp.sum(gathered, axis=0)


def squares(field):
    return jnp.sum(field * field, axis=1)


def per_device(observed, blocks, block_rows, block_cols, counts):
    tile_stack = blocks[0]
    rows_idx = block_rows[0]
    cols_idx = block_cols[0]
    slot_ids = jnp.arange(tile_stack.shape[0])
    live_slot = (slot_ids < counts[0]).astype(jnp.float32)
    axes = ("row", "col")

    def backward(field):
        return transpose_apply(field, tile_stack, rows_idx, cols_idx, live_slot)

    def forward(vector):
        return forward_apply(vector, tile_stack, rows_idx, cols_idx, live_slot)

    start_raw = backward(observed)
    totals = all_sum(jnp.stack([squares(observed), squares(start_raw)]), axes)
    row_norm = jnp.sqrt(totals[0] + 1e-06)
    col_norm = jnp.sqrt(totals[1] / (row_norm * row_norm) + 1e-06)
    scale = row_norm * col_norm
    left_vec = observed / row_norm[:, None]
    right_vec = start_raw / scale[:, None]
    left_prod = forward(start_raw)
    left_raw = left_prod / scale[:, None] - col_norm[:, None] * left_vec
    dir_now = right_vec
    solution = jnp.zeros_like(dir_now)
    phi_bar = row_norm
    diag_bar = col_norm
    for iteration in range(ITERATIONS):
        right_prod = backward(left_raw)
        row_norm = jnp.sqrt(all_sum(squares(left_raw), axes) + 1e-06)
        left_vec = left_raw / row_norm[:, None]
        right_raw = right_prod / row_norm[:, None] - row_norm[:, None] * right_vec
        if iteration + 1 < ITERATIONS:
            left_prod = forward(right_raw)
        col_norm = jnp.sqrt(all_sum(squares(right_raw), axes) + 1e-06)
        right_vec = right_raw / col_norm[:, None]
        if iteration + 1 < ITERATIONS:
            left_raw = left_prod / col_norm[:, None] - col_norm[:, None] * left_vec
        diag_new = jnp.sqrt(diag_bar * diag_bar + row_norm * row_norm)
        rot_cosine = diag_bar / diag_new
        rot_sine = row_norm / diag_new
        off_diag = rot_sine * col_norm
        diag_bar = -rot_cosine * col_norm
        phi_now = rot_cosine * phi_bar
        phi_bar = rot_sine * phi_bar
        solution = solution + (phi_now / diag_new)[:, None] * dir_now
        dir_now = right_vec - (off_diag / diag_new)[:, None] * dir_now
    return (solution, dir_now)


def solution(mesh):
    in_specs = (
        P("group", ("row", "col")),
        P(("group", "row", "col"), None, None, None),
        P(("group", "row", "col"), None),
        P(("group", "row", "col"), None),
        P(("group", "row", "col")),
    )
    out_specs = (P("group", ("row", "col")), P("group", ("row", "col")))
    return jax.shard_map(
        per_device, mesh=mesh, in_specs=in_specs, out_specs=out_specs, check_vma=False
    )
```

```python
import jax
import jax.numpy as jnp
from jax import lax
from jax.sharding import PartitionSpec as P
from jax.experimental import pallas as pl
from jax.experimental.pallas import tpu as pltpu

ROW_BLOCKS = 32
COL_BLOCKS = 64
ITERATIONS = 2


PRECISE = lax.Precision.HIGHEST
PRODUCT_PRECISION = lax.Precision.HIGH


def with_halo(shard, sides, width):
    for axis, dim in sides:
        peers, length = (lax.axis_size(axis), shard.shape[dim])
        up = [(i, (i + 1) % peers) for i in range(peers - 1)]
        down = [(j, i) for i, j in up]
        last = lax.slice_in_dim(shard, length - width, length, axis=dim)
        leading = lax.slice_in_dim(shard, 0, width, axis=dim)
        before = lax.ppermute(last, axis, up)
        after = lax.ppermute(leading, axis, down)
        shard = jnp.concatenate([before, shard, after], axis=dim)
    return shard


def from_behind(shard, axis, by):
    peers = lax.axis_size(axis)
    pairs = [(i, i + by) for i in range(peers) if 0 <= i + by < peers]
    return lax.ppermute(shard, axis, pairs)


def transpose_blocks(tile_stack, anchor):
    slots, edge, _ = tile_stack.shape
    step = 32 if slots % 32 == 0 else 1

    def body(anchor_ref, x_ref, o_ref):
        for i in range(step):
            o_ref[i] = x_ref[i].T

    nbytes = 2 * tile_stack.size * tile_stack.dtype.itemsize
    return pl.pallas_call(
        body,
        grid=(slots // step,),
        in_specs=[
            pl.BlockSpec(memory_space=pltpu.SMEM),
            pl.BlockSpec((step, edge, edge), lambda k: (k, 0, 0)),
        ],
        out_specs=pl.BlockSpec((step, edge, edge), lambda k: (k, 0, 0)),
        out_shape=jax.ShapeDtypeStruct(tile_stack.shape, tile_stack.dtype),
        cost_estimate=pl.CostEstimate(flops=0, transcendentals=0, bytes_accessed=nbytes),
    )(anchor, tile_stack)


def forward_local(window, tile_stack, rows_idx, cols_idx, live_slot):
    scenario_rows = window.shape[0]
    tile_edge = tile_stack.shape[1]
    pieces = window.reshape(scenario_rows, 3 * COL_BLOCKS, tile_edge)[:, cols_idx, :]
    products = (
        jnp.einsum("skj,kji->ksi", pieces, tile_stack, precision=PRODUCT_PRECISION) * live_slot[:, None, None]
    )
    onehot = (rows_idx[:, None] == jnp.arange(ROW_BLOCKS)[None, :]).astype(jnp.float32)
    summed = jnp.einsum("kr,ksi->sri", onehot, products, precision=PRODUCT_PRECISION)
    return summed.reshape(scenario_rows, ROW_BLOCKS * tile_edge)


def transpose_local(field, tile_stack, rows_idx, cols_idx, live_slot):
    scenario_rows = field.shape[0]
    tile_edge = tile_stack.shape[1]
    pieces = field.reshape(scenario_rows, ROW_BLOCKS, tile_edge)[:, rows_idx, :]
    products = (
        jnp.einsum("ski,kij->ksj", pieces, tile_stack, precision=PRODUCT_PRECISION) * live_slot[:, None, None]
    )
    onehot = (cols_idx[:, None] == jnp.arange(3 * COL_BLOCKS)[None, :]).astype(jnp.float32)
    summed = jnp.einsum("kc,ksj->scj", onehot, products, precision=PRODUCT_PRECISION)
    return summed.reshape(scenario_rows, 3 * COL_BLOCKS * tile_edge)


def forward_apply(vector, tile_stack, rows_idx, cols_idx, live_slot):
    window = with_halo(vector, ((("row", "col"), 1),), vector.shape[1])
    return forward_local(window, tile_stack, rows_idx, cols_idx, live_slot)


def transpose_apply(field, tile_stack, rows_idx, cols_idx, live_slot, beside=None):
    partial_sums = transpose_local(field, tile_stack, rows_idx, cols_idx, live_slot)
    band_width = partial_sums.shape[1] // 3
    lower = partial_sums[:, :band_width]
    middle = partial_sums[:, band_width : 2 * band_width]
    upper = partial_sums[:, 2 * band_width :]
    from_below = from_behind(upper, ("row", "col"), 1)
    from_above = from_behind(lower, ("row", "col"), -1)
    extra = None
    if beside is not None:
        extra = beside(middle[:1, :1])
        middle, extra = lax.optimization_barrier((middle, extra))
    result = middle + from_below + from_above
    return result, extra


def all_sum(values, axes):
    peers = 1
    for axis in axes:
        peers *= lax.axis_size(axis)
    spread = jnp.broadcast_to(values[None], (peers,) + values.shape)
    gathered = lax.all_to_all(spread, axes, 0, 0, tiled=True)
    return jnp.sum(gathered, axis=0)


def squares(field):
    return jnp.sum(field * field, axis=1)


def per_device(observed, blocks, block_rows, block_cols, counts):
    tile_stack = blocks[0]
    rows_idx = block_rows[0]
    cols_idx = block_cols[0]
    slot_ids = jnp.arange(tile_stack.shape[0])
    live_slot = (slot_ids < counts[0]).astype(jnp.float32)
    axes = ("row", "col")

    def backward(field):
        return transpose_apply(field, tile_stack, rows_idx, cols_idx, live_slot)[0]

    start_raw, tile_stack_t = transpose_apply(
        observed, tile_stack, rows_idx, cols_idx, live_slot,
        beside=lambda anchor: transpose_blocks(tile_stack, anchor),
    )

    def forward(vector):
        return forward_apply(vector, tile_stack_t, rows_idx, cols_idx, live_slot)

    totals = all_sum(jnp.stack([squares(observed), squares(start_raw)]), axes)
    row_norm = jnp.sqrt(totals[0] + 1e-06)
    col_norm = jnp.sqrt(totals[1] / (row_norm * row_norm) + 1e-06)
    scale = row_norm * col_norm
    left_vec = observed / row_norm[:, None]
    right_vec = start_raw / scale[:, None]
    left_prod = forward(start_raw)
    left_raw = left_prod / scale[:, None] - col_norm[:, None] * left_vec
    dir_now = right_vec
    solution = jnp.zeros_like(dir_now)
    phi_bar = row_norm
    diag_bar = col_norm
    for iteration in range(ITERATIONS):
        right_prod = backward(left_raw)
        row_norm = jnp.sqrt(all_sum(squares(left_raw), axes) + 1e-06)
        left_vec = left_raw / row_norm[:, None]
        right_raw = right_prod / row_norm[:, None] - row_norm[:, None] * right_vec
        if iteration + 1 < ITERATIONS:
            left_prod = forward(right_raw)
        col_norm = jnp.sqrt(all_sum(squares(right_raw), axes) + 1e-06)
        right_vec = right_raw / col_norm[:, None]
        if iteration + 1 < ITERATIONS:
            left_raw = left_prod / col_norm[:, None] - col_norm[:, None] * left_vec
        diag_new = jnp.sqrt(diag_bar * diag_bar + row_norm * row_norm)
        rot_cosine = diag_bar / diag_new
        rot_sine = row_norm / diag_new
        off_diag = rot_sine * col_norm
        diag_bar = -rot_cosine * col_norm
        phi_now = rot_cosine * phi_bar
        phi_bar = rot_sine * phi_bar
        solution = solution + (phi_now / diag_new)[:, None] * dir_now
        dir_now = right_vec - (off_diag / diag_new)[:, None] * dir_now
    return (solution, dir_now)


def solution(mesh):
    in_specs = (
        P("group", ("row", "col")),
        P(("group", "row", "col"), None, None, None),
        P(("group", "row", "col"), None),
        P(("group", "row", "col"), None),
        P(("group", "row", "col")),
    )
    out_specs = (P("group", ("row", "col")), P("group", ("row", "col")))
    return jax.shard_map(
        per_device, mesh=mesh, in_specs=in_specs, out_specs=out_specs, check_vma=False
    )
```

```python
import jax
import jax.numpy as jnp
from jax import lax
from jax.sharding import PartitionSpec as P
from jax.experimental import pallas as pl
from jax.experimental.pallas import tpu as pltpu

ROW_BLOCKS = 32
COL_BLOCKS = 64
ITERATIONS = 2


PRECISE = lax.Precision.HIGHEST
PRODUCT_PRECISION = lax.Precision.HIGH


def with_halo(shard, sides, width):
    for axis, dim in sides:
        peers, length = (lax.axis_size(axis), shard.shape[dim])
        up = [(i, (i + 1) % peers) for i in range(peers - 1)]
        down = [(j, i) for i, j in up]
        last = lax.slice_in_dim(shard, length - width, length, axis=dim)
        leading = lax.slice_in_dim(shard, 0, width, axis=dim)
        before = lax.ppermute(last, axis, up)
        after = lax.ppermute(leading, axis, down)
        shard = jnp.concatenate([before, shard, after], axis=dim)
    return shard


def from_behind(shard, axis, by):
    peers = lax.axis_size(axis)
    pairs = [(i, i + by) for i in range(peers) if 0 <= i + by < peers]
    return lax.ppermute(shard, axis, pairs)


def transpose_blocks(tile_stack, anchor, first, count, into=None):
    slots, edge, _ = tile_stack.shape
    step = 16 if count % 16 == 0 and first % 16 == 0 else 1
    offset = first // step

    def body(anchor_ref, x_ref, *refs):
        o_ref = refs[-1]
        for i in range(step):
            o_ref[i] = x_ref[i].T

    in_specs = [
        pl.BlockSpec(memory_space=pltpu.SMEM),
        pl.BlockSpec((step, edge, edge), lambda k: (k + offset, 0, 0)),
    ]
    operands = [anchor, tile_stack]
    aliases = {}
    if into is not None:
        in_specs.append(pl.BlockSpec(memory_space=pl.ANY))
        operands.append(into)
        aliases = {2: 0}
    nbytes = 2 * count * edge * edge * tile_stack.dtype.itemsize
    return pl.pallas_call(
        body,
        grid=(count // step,),
        in_specs=in_specs,
        out_specs=pl.BlockSpec((step, edge, edge), lambda k: (k + offset, 0, 0)),
        out_shape=jax.ShapeDtypeStruct(tile_stack.shape, tile_stack.dtype),
        input_output_aliases=aliases,
        cost_estimate=pl.CostEstimate(flops=0, transcendentals=0, bytes_accessed=nbytes),
    )(*operands)


def forward_local(window, tile_stack, rows_idx, cols_idx, live_slot):
    scenario_rows = window.shape[0]
    tile_edge = tile_stack.shape[1]
    pieces = window.reshape(scenario_rows, 3 * COL_BLOCKS, tile_edge)[:, cols_idx, :]
    products = (
        jnp.einsum("skj,kji->ksi", pieces, tile_stack, precision=PRODUCT_PRECISION) * live_slot[:, None, None]
    )
    onehot = (rows_idx[:, None] == jnp.arange(ROW_BLOCKS)[None, :]).astype(jnp.float32)
    summed = jnp.einsum("kr,ksi->sri", onehot, products, precision=PRODUCT_PRECISION)
    return summed.reshape(scenario_rows, ROW_BLOCKS * tile_edge)


def transpose_local(field, tile_stack, rows_idx, cols_idx, live_slot):
    scenario_rows = field.shape[0]
    tile_edge = tile_stack.shape[1]
    pieces = field.reshape(scenario_rows, ROW_BLOCKS, tile_edge)[:, rows_idx, :]
    products = (
        jnp.einsum("ski,kij->ksj", pieces, tile_stack, precision=PRODUCT_PRECISION) * live_slot[:, None, None]
    )
    onehot = (cols_idx[:, None] == jnp.arange(3 * COL_BLOCKS)[None, :]).astype(jnp.float32)
    summed = jnp.einsum("kc,ksj->scj", onehot, products, precision=PRODUCT_PRECISION)
    return summed.reshape(scenario_rows, 3 * COL_BLOCKS * tile_edge)


def forward_apply(vector, tile_stack, rows_idx, cols_idx, live_slot):
    window = with_halo(vector, ((("row", "col"), 1),), vector.shape[1])
    return forward_local(window, tile_stack, rows_idx, cols_idx, live_slot)


def transpose_apply(field, tile_stack, rows_idx, cols_idx, live_slot, beside=None):
    partial_sums = transpose_local(field, tile_stack, rows_idx, cols_idx, live_slot)
    band_width = partial_sums.shape[1] // 3
    lower = partial_sums[:, :band_width]
    middle = partial_sums[:, band_width : 2 * band_width]
    upper = partial_sums[:, 2 * band_width :]
    from_below = from_behind(upper, ("row", "col"), 1)
    from_above = from_behind(lower, ("row", "col"), -1)
    extra = None
    if beside is not None:
        extra = beside(middle[:1, :1])
        middle, extra = lax.optimization_barrier((middle, extra))
    result = middle + from_below + from_above
    return result, extra


def all_sum(values, axes):
    peers = 1
    for axis in axes:
        peers *= lax.axis_size(axis)
    spread = jnp.broadcast_to(values[None], (peers,) + values.shape)
    gathered = lax.all_to_all(spread, axes, 0, 0, tiled=True)
    return jnp.sum(gathered, axis=0)


def squares(field):
    return jnp.sum(field * field, axis=1)


def per_device(observed, blocks, block_rows, block_cols, counts):
    tile_stack = blocks[0]
    rows_idx = block_rows[0]
    cols_idx = block_cols[0]
    slot_ids = jnp.arange(tile_stack.shape[0])
    live_slot = (slot_ids < counts[0]).astype(jnp.float32)
    axes = ("row", "col")

    def backward(field):
        return transpose_apply(field, tile_stack, rows_idx, cols_idx, live_slot)[0]

    slots = tile_stack.shape[0]
    half = slots // 2
    start_raw, first_half = transpose_apply(
        observed, tile_stack, rows_idx, cols_idx, live_slot,
        beside=lambda anchor: transpose_blocks(tile_stack, anchor, 0, half),
    )
    tile_stack_t = transpose_blocks(tile_stack, start_raw[:1, :1], half, slots - half, into=first_half)

    def forward(vector):
        return forward_apply(vector, tile_stack_t, rows_idx, cols_idx, live_slot)

    totals = all_sum(jnp.stack([squares(observed), squares(start_raw)]), axes)
    row_norm = jnp.sqrt(totals[0] + 1e-06)
    col_norm = jnp.sqrt(totals[1] / (row_norm * row_norm) + 1e-06)
    scale = row_norm * col_norm
    left_vec = observed / row_norm[:, None]
    right_vec = start_raw / scale[:, None]
    left_prod = forward(start_raw)
    left_raw = left_prod / scale[:, None] - col_norm[:, None] * left_vec
    dir_now = right_vec
    solution = jnp.zeros_like(dir_now)
    phi_bar = row_norm
    diag_bar = col_norm
    for iteration in range(ITERATIONS):
        right_prod = backward(left_raw)
        row_norm = jnp.sqrt(all_sum(squares(left_raw), axes) + 1e-06)
        left_vec = left_raw / row_norm[:, None]
        right_raw = right_prod / row_norm[:, None] - row_norm[:, None] * right_vec
        if iteration + 1 < ITERATIONS:
            left_prod = forward(right_raw)
        col_norm = jnp.sqrt(all_sum(squares(right_raw), axes) + 1e-06)
        right_vec = right_raw / col_norm[:, None]
        if iteration + 1 < ITERATIONS:
            left_raw = left_prod / col_norm[:, None] - col_norm[:, None] * left_vec
        diag_new = jnp.sqrt(diag_bar * diag_bar + row_norm * row_norm)
        rot_cosine = diag_bar / diag_new
        rot_sine = row_norm / diag_new
        off_diag = rot_sine * col_norm
        diag_bar = -rot_cosine * col_norm
        phi_now = rot_cosine * phi_bar
        phi_bar = rot_sine * phi_bar
        solution = solution + (phi_now / diag_new)[:, None] * dir_now
        dir_now = right_vec - (off_diag / diag_new)[:, None] * dir_now
    return (solution, dir_now)


def solution(mesh):
    in_specs = (
        P("group", ("row", "col")),
        P(("group", "row", "col"), None, None, None),
        P(("group", "row", "col"), None),
        P(("group", "row", "col"), None),
        P(("group", "row", "col")),
    )
    out_specs = (P("group", ("row", "col")), P("group", ("row", "col")))
    return jax.shard_map(
        per_device, mesh=mesh, in_specs=in_specs, out_specs=out_specs, check_vma=False
    )
```

```python
import jax
import jax.numpy as jnp
from jax import lax
from jax.sharding import PartitionSpec as P
from jax.experimental import pallas as pl
from jax.experimental.pallas import tpu as pltpu

ROW_BLOCKS = 32
COL_BLOCKS = 64
ITERATIONS = 2


PRECISE = lax.Precision.HIGHEST
PRODUCT_PRECISION = lax.Precision.HIGH


def with_halo(shard, sides, width):
    for axis, dim in sides:
        peers, length = (lax.axis_size(axis), shard.shape[dim])
        up = [(i, (i + 1) % peers) for i in range(peers - 1)]
        down = [(j, i) for i, j in up]
        last = lax.slice_in_dim(shard, length - width, length, axis=dim)
        leading = lax.slice_in_dim(shard, 0, width, axis=dim)
        before = lax.ppermute(last, axis, up)
        after = lax.ppermute(leading, axis, down)
        shard = jnp.concatenate([before, shard, after], axis=dim)
    return shard


def from_behind(shard, axis, by):
    peers = lax.axis_size(axis)
    pairs = [(i, i + by) for i in range(peers) if 0 <= i + by < peers]
    return lax.ppermute(shard, axis, pairs)


def transpose_blocks(tile_stack, anchor):
    slots, edge, _ = tile_stack.shape
    step = 32 if slots % 32 == 0 else 1

    def body(anchor_ref, x_ref, o_ref):
        for i in range(step):
            o_ref[i] = x_ref[i].T

    nbytes = 2 * tile_stack.size * tile_stack.dtype.itemsize
    return pl.pallas_call(
        body,
        grid=(slots // step,),
        in_specs=[
            pl.BlockSpec(memory_space=pltpu.SMEM),
            pl.BlockSpec((step, edge, edge), lambda k: (k, 0, 0)),
        ],
        out_specs=pl.BlockSpec((step, edge, edge), lambda k: (k, 0, 0)),
        out_shape=jax.ShapeDtypeStruct(tile_stack.shape, tile_stack.dtype),
        cost_estimate=pl.CostEstimate(flops=0, transcendentals=0, bytes_accessed=nbytes),
    )(anchor, tile_stack)


def forward_local(window, tile_stack_t, rows_idx, cols_idx, live_slot):
    pieces = window[cols_idx]
    products = (
        jnp.einsum("ksj,kji->ksi", pieces, tile_stack_t, precision=PRODUCT_PRECISION)
        * live_slot[:, None, None]
    )
    onehot = (rows_idx[:, None] == jnp.arange(ROW_BLOCKS)[None, :]).astype(jnp.float32)
    return jnp.einsum("kr,ksi->rsi", onehot, products, precision=PRODUCT_PRECISION)


def transpose_local(field, tile_stack, rows_idx, cols_idx, live_slot):
    pieces = field[rows_idx]
    products = (
        jnp.einsum("ksi,kij->ksj", pieces, tile_stack, precision=PRODUCT_PRECISION)
        * live_slot[:, None, None]
    )
    onehot = (cols_idx[:, None] == jnp.arange(3 * COL_BLOCKS)[None, :]).astype(jnp.float32)
    return jnp.einsum("kc,ksj->csj", onehot, products, precision=PRODUCT_PRECISION)


def forward_apply(vector, tile_stack_t, rows_idx, cols_idx, live_slot):
    window = with_halo(vector, ((("row", "col"), 0),), vector.shape[0])
    return forward_local(window, tile_stack_t, rows_idx, cols_idx, live_slot)


def transpose_apply(field, tile_stack, rows_idx, cols_idx, live_slot, beside=None):
    partial_sums = transpose_local(field, tile_stack, rows_idx, cols_idx, live_slot)
    band = partial_sums.shape[0] // 3
    lower = partial_sums[:band]
    middle = partial_sums[band : 2 * band]
    upper = partial_sums[2 * band :]
    from_below = from_behind(upper, ("row", "col"), 1)
    from_above = from_behind(lower, ("row", "col"), -1)
    extra = None
    if beside is not None:
        extra = beside(middle[:1, :1, 0])
        middle, extra = lax.optimization_barrier((middle, extra))
    result = middle + from_below + from_above
    return result, extra


def all_sum(values, axes):
    peers = 1
    for axis in axes:
        peers *= lax.axis_size(axis)
    spread = jnp.broadcast_to(values[None], (peers,) + values.shape)
    gathered = lax.all_to_all(spread, axes, 0, 0, tiled=True)
    return jnp.sum(gathered, axis=0)


def squares(field):
    return jnp.sum(field * field, axis=(0, 2))


def per_row(values):
    return values[None, :, None]


def per_device(observed, blocks, block_rows, block_cols, counts):
    tile_stack = blocks[0]
    rows_idx = block_rows[0]
    cols_idx = block_cols[0]
    slot_ids = jnp.arange(tile_stack.shape[0])
    live_slot = (slot_ids < counts[0]).astype(jnp.float32)
    axes = ("row", "col")
    scenarios, rows_here = observed.shape
    edge = tile_stack.shape[1]
    observed = jnp.swapaxes(observed.reshape(scenarios, rows_here // edge, edge), 0, 1)

    def backward(field):
        return transpose_apply(field, tile_stack, rows_idx, cols_idx, live_slot)[0]

    start_raw, tile_stack_t = transpose_apply(
        observed, tile_stack, rows_idx, cols_idx, live_slot,
        beside=lambda anchor: transpose_blocks(tile_stack, anchor),
    )

    def forward(vector):
        return forward_apply(vector, tile_stack_t, rows_idx, cols_idx, live_slot)

    totals = all_sum(jnp.stack([squares(observed), squares(start_raw)]), axes)
    row_norm = jnp.sqrt(totals[0] + 1e-06)
    col_norm = jnp.sqrt(totals[1] / (row_norm * row_norm) + 1e-06)
    scale = row_norm * col_norm
    left_vec = observed / per_row(row_norm)
    right_vec = start_raw / per_row(scale)
    left_prod = forward(start_raw)
    left_raw = left_prod / per_row(scale) - per_row(col_norm) * left_vec
    dir_now = right_vec
    solution = jnp.zeros_like(dir_now)
    phi_bar = row_norm
    diag_bar = col_norm
    for iteration in range(ITERATIONS):
        right_prod = backward(left_raw)
        row_norm = jnp.sqrt(all_sum(squares(left_raw), axes) + 1e-06)
        left_vec = left_raw / per_row(row_norm)
        right_raw = right_prod / per_row(row_norm) - per_row(row_norm) * right_vec
        if iteration + 1 < ITERATIONS:
            left_prod = forward(right_raw)
        col_norm = jnp.sqrt(all_sum(squares(right_raw), axes) + 1e-06)
        right_vec = right_raw / per_row(col_norm)
        if iteration + 1 < ITERATIONS:
            left_raw = left_prod / per_row(col_norm) - per_row(col_norm) * left_vec
        diag_new = jnp.sqrt(diag_bar * diag_bar + row_norm * row_norm)
        rot_cosine = diag_bar / diag_new
        rot_sine = row_norm / diag_new
        off_diag = rot_sine * col_norm
        diag_bar = -rot_cosine * col_norm
        phi_now = rot_cosine * phi_bar
        phi_bar = rot_sine * phi_bar
        solution = solution + per_row(phi_now / diag_new) * dir_now
        dir_now = right_vec - per_row(off_diag / diag_new) * dir_now

    def rows_major(field):
        return jnp.swapaxes(field, 0, 1).reshape(scenarios, -1)

    return (rows_major(solution), rows_major(dir_now))


def solution(mesh):
    in_specs = (
        P("group", ("row", "col")),
        P(("group", "row", "col"), None, None, None),
        P(("group", "row", "col"), None),
        P(("group", "row", "col"), None),
        P(("group", "row", "col")),
    )
    out_specs = (P("group", ("row", "col")), P("group", ("row", "col")))
    return jax.shard_map(
        per_device, mesh=mesh, in_specs=in_specs, out_specs=out_specs, check_vma=False
    )
```

```python
import jax
import jax.numpy as jnp
from jax import lax
from jax.sharding import PartitionSpec as P
from jax.experimental import pallas as pl
from jax.experimental.pallas import tpu as pltpu

ROW_BLOCKS = 32
COL_BLOCKS = 64
ITERATIONS = 2


PRECISE = lax.Precision.HIGHEST
PRODUCT_PRECISION = lax.Precision.HIGH


def with_halo(shard, sides, width):
    for axis, dim in sides:
        peers, length = (lax.axis_size(axis), shard.shape[dim])
        up = [(i, (i + 1) % peers) for i in range(peers - 1)]
        down = [(j, i) for i, j in up]
        last = lax.slice_in_dim(shard, length - width, length, axis=dim)
        leading = lax.slice_in_dim(shard, 0, width, axis=dim)
        before = lax.ppermute(last, axis, up)
        after = lax.ppermute(leading, axis, down)
        shard = jnp.concatenate([before, shard, after], axis=dim)
    return shard


def from_behind(shard, axis, by):
    peers = lax.axis_size(axis)
    pairs = [(i, i + by) for i in range(peers) if 0 <= i + by < peers]
    return lax.ppermute(shard, axis, pairs)


def transpose_blocks(tile_stack, anchor):
    slots, edge, _ = tile_stack.shape
    step = 80 if slots % 80 == 0 else (32 if slots % 32 == 0 else 1)

    def body(anchor_ref, x_ref, o_ref):
        for i in range(step):
            o_ref[i] = x_ref[i].T

    nbytes = 2 * tile_stack.size * tile_stack.dtype.itemsize
    return pl.pallas_call(
        body,
        grid=(slots // step,),
        in_specs=[
            pl.BlockSpec(memory_space=pltpu.SMEM),
            pl.BlockSpec((step, edge, edge), lambda k: (k, 0, 0)),
        ],
        out_specs=pl.BlockSpec((step, edge, edge), lambda k: (k, 0, 0)),
        out_shape=jax.ShapeDtypeStruct(tile_stack.shape, tile_stack.dtype),
        cost_estimate=pl.CostEstimate(flops=0, transcendentals=0, bytes_accessed=nbytes),
    )(anchor, tile_stack)


def forward_local(window, tile_stack, rows_idx, cols_idx, live_slot):
    scenario_rows = window.shape[0]
    tile_edge = tile_stack.shape[1]
    pieces = window.reshape(scenario_rows, 3 * COL_BLOCKS, tile_edge)[:, cols_idx, :]
    products = (
        jnp.einsum("skj,kji->ksi", pieces, tile_stack, precision=PRODUCT_PRECISION) * live_slot[:, None, None]
    )
    onehot = (rows_idx[:, None] == jnp.arange(ROW_BLOCKS)[None, :]).astype(jnp.float32)
    summed = jnp.einsum("kr,ksi->sri", onehot, products, precision=PRODUCT_PRECISION)
    return summed.reshape(scenario_rows, ROW_BLOCKS * tile_edge)


def transpose_local(field, tile_stack, rows_idx, cols_idx, live_slot):
    scenario_rows = field.shape[0]
    tile_edge = tile_stack.shape[1]
    pieces = field.reshape(scenario_rows, ROW_BLOCKS, tile_edge)[:, rows_idx, :]
    products = (
        jnp.einsum("ski,kij->ksj", pieces, tile_stack, precision=PRODUCT_PRECISION) * live_slot[:, None, None]
    )
    onehot = (cols_idx[:, None] == jnp.arange(3 * COL_BLOCKS)[None, :]).astype(jnp.float32)
    summed = jnp.einsum("kc,ksj->scj", onehot, products, precision=PRODUCT_PRECISION)
    return summed.reshape(scenario_rows, 3 * COL_BLOCKS * tile_edge)


def forward_apply(vector, tile_stack, rows_idx, cols_idx, live_slot):
    window = with_halo(vector, ((("row", "col"), 1),), vector.shape[1])
    return forward_local(window, tile_stack, rows_idx, cols_idx, live_slot)


def transpose_apply(field, tile_stack, rows_idx, cols_idx, live_slot, beside=None):
    partial_sums = transpose_local(field, tile_stack, rows_idx, cols_idx, live_slot)
    band_width = partial_sums.shape[1] // 3
    lower = partial_sums[:, :band_width]
    middle = partial_sums[:, band_width : 2 * band_width]
    upper = partial_sums[:, 2 * band_width :]
    from_below = from_behind(upper, ("row", "col"), 1)
    from_above = from_behind(lower, ("row", "col"), -1)
    extra = None
    if beside is not None:
        extra = beside(middle[:1, :1])
        middle, extra = lax.optimization_barrier((middle, extra))
    result = middle + from_below + from_above
    return result, extra


def all_sum(values, axes):
    peers = 1
    for axis in axes:
        peers *= lax.axis_size(axis)
    spread = jnp.broadcast_to(values[None], (peers,) + values.shape)
    gathered = lax.all_to_all(spread, axes, 0, 0, tiled=True)
    return jnp.sum(gathered, axis=0)


def squares(field):
    return jnp.sum(field * field, axis=1)


def per_device(observed, blocks, block_rows, block_cols, counts):
    tile_stack = blocks[0]
    rows_idx = block_rows[0]
    cols_idx = block_cols[0]
    slot_ids = jnp.arange(tile_stack.shape[0])
    live_slot = (slot_ids < counts[0]).astype(jnp.float32)
    axes = ("row", "col")

    def backward(field):
        return transpose_apply(field, tile_stack, rows_idx, cols_idx, live_slot)[0]

    start_raw, tile_stack_t = transpose_apply(
        observed, tile_stack, rows_idx, cols_idx, live_slot,
        beside=lambda anchor: transpose_blocks(tile_stack, anchor),
    )

    def forward(vector):
        return forward_apply(vector, tile_stack_t, rows_idx, cols_idx, live_slot)

    totals = all_sum(jnp.stack([squares(observed), squares(start_raw)]), axes)
    row_norm = jnp.sqrt(totals[0] + 1e-06)
    col_norm = jnp.sqrt(totals[1] / (row_norm * row_norm) + 1e-06)
    scale = row_norm * col_norm
    left_vec = observed / row_norm[:, None]
    right_vec = start_raw / scale[:, None]
    left_prod = forward(start_raw)
    left_raw = left_prod / scale[:, None] - col_norm[:, None] * left_vec
    dir_now = right_vec
    solution = jnp.zeros_like(dir_now)
    phi_bar = row_norm
    diag_bar = col_norm
    for iteration in range(ITERATIONS):
        right_prod = backward(left_raw)
        row_norm = jnp.sqrt(all_sum(squares(left_raw), axes) + 1e-06)
        left_vec = left_raw / row_norm[:, None]
        right_raw = right_prod / row_norm[:, None] - row_norm[:, None] * right_vec
        if iteration + 1 < ITERATIONS:
            left_prod = forward(right_raw)
        col_norm = jnp.sqrt(all_sum(squares(right_raw), axes) + 1e-06)
        right_vec = right_raw / col_norm[:, None]
        if iteration + 1 < ITERATIONS:
            left_raw = left_prod / col_norm[:, None] - col_norm[:, None] * left_vec
        diag_new = jnp.sqrt(diag_bar * diag_bar + row_norm * row_norm)
        rot_cosine = diag_bar / diag_new
        rot_sine = row_norm / diag_new
        off_diag = rot_sine * col_norm
        diag_bar = -rot_cosine * col_norm
        phi_now = rot_cosine * phi_bar
        phi_bar = rot_sine * phi_bar
        solution = solution + (phi_now / diag_new)[:, None] * dir_now
        dir_now = right_vec - (off_diag / diag_new)[:, None] * dir_now
    return (solution, dir_now)


def solution(mesh):
    in_specs = (
        P("group", ("row", "col")),
        P(("group", "row", "col"), None, None, None),
        P(("group", "row", "col"), None),
        P(("group", "row", "col"), None),
        P(("group", "row", "col")),
    )
    out_specs = (P("group", ("row", "col")), P("group", ("row", "col")))
    return jax.shard_map(
        per_device, mesh=mesh, in_specs=in_specs, out_specs=out_specs, check_vma=False
    )
```

```python
import jax
import jax.numpy as jnp
from jax import lax
from jax.sharding import PartitionSpec as P
from jax.experimental import pallas as pl
from jax.experimental.pallas import tpu as pltpu

ROW_BLOCKS = 32
COL_BLOCKS = 64
ITERATIONS = 2


PRECISE = lax.Precision.HIGHEST
PRODUCT_PRECISION = lax.Precision.HIGH


def with_halo(shard, sides, width):
    for axis, dim in sides:
        peers, length = (lax.axis_size(axis), shard.shape[dim])
        up = [(i, (i + 1) % peers) for i in range(peers - 1)]
        down = [(j, i) for i, j in up]
        last = lax.slice_in_dim(shard, length - width, length, axis=dim)
        leading = lax.slice_in_dim(shard, 0, width, axis=dim)
        before = lax.ppermute(last, axis, up)
        after = lax.ppermute(leading, axis, down)
        shard = jnp.concatenate([before, shard, after], axis=dim)
    return shard


def from_behind(shard, axis, by):
    peers = lax.axis_size(axis)
    pairs = [(i, i + by) for i in range(peers) if 0 <= i + by < peers]
    return lax.ppermute(shard, axis, pairs)


def transpose_blocks(tile_stack, anchor):
    slots, edge, _ = tile_stack.shape
    step = 80 if slots % 80 == 0 else (32 if slots % 32 == 0 else 1)

    def body(anchor_ref, x_ref, o_ref):
        for i in range(step):
            o_ref[i] = x_ref[i].T

    nbytes = 2 * tile_stack.size * tile_stack.dtype.itemsize
    return pl.pallas_call(
        body,
        grid=(slots // step,),
        in_specs=[
            pl.BlockSpec(memory_space=pltpu.SMEM),
            pl.BlockSpec((step, edge, edge), lambda k: (k, 0, 0)),
        ],
        out_specs=pl.BlockSpec((step, edge, edge), lambda k: (k, 0, 0)),
        out_shape=jax.ShapeDtypeStruct(tile_stack.shape, tile_stack.dtype),
        cost_estimate=pl.CostEstimate(flops=0, transcendentals=0, bytes_accessed=nbytes),
    )(anchor, tile_stack)


def forward_local(window, tile_stack, rows_idx, cols_idx, live_slot):
    scenario_rows = window.shape[0]
    tile_edge = tile_stack.shape[1]
    pieces = window.reshape(scenario_rows, 3 * COL_BLOCKS, tile_edge)[:, cols_idx, :]
    products = (
        jnp.einsum("skj,kji->ksi", pieces, tile_stack, precision=PRODUCT_PRECISION) * live_slot[:, None, None]
    )
    onehot = (rows_idx[:, None] == jnp.arange(ROW_BLOCKS)[None, :]).astype(jnp.float32)
    summed = jnp.einsum("kr,ksi->sri", onehot, products, precision=PRODUCT_PRECISION)
    return summed.reshape(scenario_rows, ROW_BLOCKS * tile_edge)


def transpose_local(field, tile_stack, rows_idx, cols_idx, live_slot):
    scenario_rows = field.shape[0]
    tile_edge = tile_stack.shape[1]
    pieces = field.reshape(scenario_rows, ROW_BLOCKS, tile_edge)[:, rows_idx, :]
    products = (
        jnp.einsum("ski,kij->ksj", pieces, tile_stack, precision=PRODUCT_PRECISION) * live_slot[:, None, None]
    )
    onehot = (cols_idx[:, None] == jnp.arange(3 * COL_BLOCKS)[None, :]).astype(jnp.float32)
    summed = jnp.einsum("kc,ksj->scj", onehot, products, precision=PRODUCT_PRECISION)
    return summed.reshape(scenario_rows, 3 * COL_BLOCKS * tile_edge)


def forward_apply(vector, tile_stack, rows_idx, cols_idx, live_slot):
    window = with_halo(vector, ((("row", "col"), 1),), vector.shape[1])
    return forward_local(window, tile_stack, rows_idx, cols_idx, live_slot)


def transpose_apply(field, tile_stack, rows_idx, cols_idx, live_slot, beside=None):
    partial_sums = transpose_local(field, tile_stack, rows_idx, cols_idx, live_slot)
    band_width = partial_sums.shape[1] // 3
    lower = partial_sums[:, :band_width]
    middle = partial_sums[:, band_width : 2 * band_width]
    upper = partial_sums[:, 2 * band_width :]
    from_below = from_behind(upper, ("row", "col"), 1)
    from_above = from_behind(lower, ("row", "col"), -1)
    extra = None
    if beside is not None:
        extra = beside(middle[:1, :1])
        middle, extra = lax.optimization_barrier((middle, extra))
    result = middle + from_below + from_above
    return result, extra


def all_sum(values, axes):
    peers = 1
    for axis in axes:
        peers *= lax.axis_size(axis)
    spread = jnp.broadcast_to(values[None], (peers,) + values.shape)
    gathered = lax.all_to_all(spread, axes, 0, 0, tiled=True)
    return jnp.sum(gathered, axis=0)


def squares(field):
    return jnp.sum(field * field, axis=1)


def per_device(observed, blocks, block_rows, block_cols, counts):
    tile_stack = blocks[0]
    rows_idx = block_rows[0]
    cols_idx = block_cols[0]
    slot_ids = jnp.arange(tile_stack.shape[0])
    live_slot = (slot_ids < counts[0]).astype(jnp.float32)
    axes = ("row", "col")

    def backward(field):
        return transpose_apply(field, tile_stack, rows_idx, cols_idx, live_slot)[0]

    start_raw, tile_stack_t = transpose_apply(
        observed, tile_stack, rows_idx, cols_idx, live_slot,
        beside=lambda anchor: transpose_blocks(tile_stack, anchor),
    )

    def halo(vector):
        return with_halo(vector, ((axes, 1),), vector.shape[1])

    def forward_window(window):
        return forward_local(window, tile_stack_t, rows_idx, cols_idx, live_slot)

    totals = all_sum(jnp.stack([squares(observed), squares(start_raw)]), axes)
    row_norm = jnp.sqrt(totals[0] + 1e-06)
    col_norm = jnp.sqrt(totals[1] / (row_norm * row_norm) + 1e-06)
    scale = row_norm * col_norm
    left_vec = observed / row_norm[:, None]
    right_vec = start_raw / scale[:, None]
    start_window = halo(start_raw)
    left_prod = forward_window(start_window)
    right_window = start_window / scale[:, None]
    left_raw = left_prod / scale[:, None] - col_norm[:, None] * left_vec
    dir_now = right_vec
    solution = jnp.zeros_like(dir_now)
    phi_bar = row_norm
    diag_bar = col_norm
    for iteration in range(ITERATIONS):
        right_prod = backward(left_raw)
        row_norm = jnp.sqrt(all_sum(squares(left_raw), axes) + 1e-06)
        left_vec = left_raw / row_norm[:, None]
        right_raw = right_prod / row_norm[:, None] - row_norm[:, None] * right_vec
        if iteration + 1 < ITERATIONS:
            raw_window = halo(right_prod) / row_norm[:, None] - row_norm[:, None] * right_window
            left_prod = forward_window(raw_window)
        col_norm = jnp.sqrt(all_sum(squares(right_raw), axes) + 1e-06)
        right_vec = right_raw / col_norm[:, None]
        if iteration + 1 < ITERATIONS:
            left_raw = left_prod / col_norm[:, None] - col_norm[:, None] * left_vec
            right_window = raw_window / col_norm[:, None]
        diag_new = jnp.sqrt(diag_bar * diag_bar + row_norm * row_norm)
        rot_cosine = diag_bar / diag_new
        rot_sine = row_norm / diag_new
        off_diag = rot_sine * col_norm
        diag_bar = -rot_cosine * col_norm
        phi_now = rot_cosine * phi_bar
        phi_bar = rot_sine * phi_bar
        solution = solution + (phi_now / diag_new)[:, None] * dir_now
        dir_now = right_vec - (off_diag / diag_new)[:, None] * dir_now
    return (solution, dir_now)


def solution(mesh):
    in_specs = (
        P("group", ("row", "col")),
        P(("group", "row", "col"), None, None, None),
        P(("group", "row", "col"), None),
        P(("group", "row", "col"), None),
        P(("group", "row", "col")),
    )
    out_specs = (P("group", ("row", "col")), P("group", ("row", "col")))
    return jax.shard_map(
        per_device, mesh=mesh, in_specs=in_specs, out_specs=out_specs, check_vma=False
    )
```

```python
import jax
import jax.numpy as jnp
from jax import lax
from jax.sharding import PartitionSpec as P
from jax.experimental import pallas as pl
from jax.experimental.pallas import tpu as pltpu

ROW_BLOCKS = 32
COL_BLOCKS = 64
ITERATIONS = 2


PRECISE = lax.Precision.HIGHEST
PRODUCT_PRECISION = lax.Precision.HIGH


def with_halo(shard, sides, width):
    for axis, dim in sides:
        peers, length = (lax.axis_size(axis), shard.shape[dim])
        up = [(i, (i + 1) % peers) for i in range(peers - 1)]
        down = [(j, i) for i, j in up]
        last = lax.slice_in_dim(shard, length - width, length, axis=dim)
        leading = lax.slice_in_dim(shard, 0, width, axis=dim)
        before = lax.ppermute(last, axis, up)
        after = lax.ppermute(leading, axis, down)
        shard = jnp.concatenate([before, shard, after], axis=dim)
    return shard


def from_behind(shard, axis, by):
    peers = lax.axis_size(axis)
    pairs = [(i, i + by) for i in range(peers) if 0 <= i + by < peers]
    return lax.ppermute(shard, axis, pairs)


def transpose_blocks(tile_stack, anchor):
    slots, edge, _ = tile_stack.shape
    step = 80 if slots % 80 == 0 else (32 if slots % 32 == 0 else 1)

    def body(anchor_ref, x_ref, o_ref):
        for i in range(step):
            o_ref[i] = x_ref[i].T

    nbytes = 2 * tile_stack.size * tile_stack.dtype.itemsize
    return pl.pallas_call(
        body,
        grid=(slots // step,),
        in_specs=[
            pl.BlockSpec(memory_space=pltpu.SMEM),
            pl.BlockSpec((step, edge, edge), lambda k: (k, 0, 0)),
        ],
        out_specs=pl.BlockSpec((step, edge, edge), lambda k: (k, 0, 0)),
        out_shape=jax.ShapeDtypeStruct(tile_stack.shape, tile_stack.dtype),
        cost_estimate=pl.CostEstimate(flops=0, transcendentals=0, bytes_accessed=nbytes),
    )(anchor, tile_stack)


def forward_local(window, tile_stack, rows_idx, cols_idx, live_slot):
    scenario_rows = window.shape[0]
    tile_edge = tile_stack.shape[1]
    pieces = window.reshape(scenario_rows, 3 * COL_BLOCKS, tile_edge)[:, cols_idx, :]
    products = (
        jnp.einsum("skj,kji->ksi", pieces, tile_stack, precision=PRODUCT_PRECISION) * live_slot[:, None, None]
    )
    summed = jnp.zeros((scenario_rows, ROW_BLOCKS, tile_edge), jnp.float32)
    summed = summed.at[:, rows_idx, :].add(jnp.swapaxes(products, 0, 1), mode="promise_in_bounds")
    return summed.reshape(scenario_rows, ROW_BLOCKS * tile_edge)


def transpose_local(field, tile_stack, rows_idx, cols_idx, live_slot):
    scenario_rows = field.shape[0]
    tile_edge = tile_stack.shape[1]
    pieces = field.reshape(scenario_rows, ROW_BLOCKS, tile_edge)[:, rows_idx, :]
    products = (
        jnp.einsum("ski,kij->ksj", pieces, tile_stack, precision=PRODUCT_PRECISION) * live_slot[:, None, None]
    )
    summed = jnp.zeros((scenario_rows, 3 * COL_BLOCKS, tile_edge), jnp.float32)
    summed = summed.at[:, cols_idx, :].add(jnp.swapaxes(products, 0, 1), mode="promise_in_bounds")
    return summed.reshape(scenario_rows, 3 * COL_BLOCKS * tile_edge)


def forward_apply(vector, tile_stack, rows_idx, cols_idx, live_slot):
    window = with_halo(vector, ((("row", "col"), 1),), vector.shape[1])
    return forward_local(window, tile_stack, rows_idx, cols_idx, live_slot)


def transpose_apply(field, tile_stack, rows_idx, cols_idx, live_slot, beside=None):
    partial_sums = transpose_local(field, tile_stack, rows_idx, cols_idx, live_slot)
    band_width = partial_sums.shape[1] // 3
    lower = partial_sums[:, :band_width]
    middle = partial_sums[:, band_width : 2 * band_width]
    upper = partial_sums[:, 2 * band_width :]
    from_below = from_behind(upper, ("row", "col"), 1)
    from_above = from_behind(lower, ("row", "col"), -1)
    extra = None
    if beside is not None:
        extra = beside(middle[:1, :1])
        middle, extra = lax.optimization_barrier((middle, extra))
    result = middle + from_below + from_above
    return result, extra


def all_sum(values, axes):
    peers = 1
    for axis in axes:
        peers *= lax.axis_size(axis)
    spread = jnp.broadcast_to(values[None], (peers,) + values.shape)
    gathered = lax.all_to_all(spread, axes, 0, 0, tiled=True)
    return jnp.sum(gathered, axis=0)


def squares(field):
    return jnp.sum(field * field, axis=1)


def per_device(observed, blocks, block_rows, block_cols, counts):
    tile_stack = blocks[0]
    rows_idx = block_rows[0]
    cols_idx = block_cols[0]
    slot_ids = jnp.arange(tile_stack.shape[0])
    live_slot = (slot_ids < counts[0]).astype(jnp.float32)
    axes = ("row", "col")

    def backward(field):
        return transpose_apply(field, tile_stack, rows_idx, cols_idx, live_slot)[0]

    start_raw, tile_stack_t = transpose_apply(
        observed, tile_stack, rows_idx, cols_idx, live_slot,
        beside=lambda anchor: transpose_blocks(tile_stack, anchor),
    )

    def forward(vector):
        return forward_apply(vector, tile_stack_t, rows_idx, cols_idx, live_slot)

    totals = all_sum(jnp.stack([squares(observed), squares(start_raw)]), axes)
    row_norm = jnp.sqrt(totals[0] + 1e-06)
    col_norm = jnp.sqrt(totals[1] / (row_norm * row_norm) + 1e-06)
    scale = row_norm * col_norm
    left_vec = observed / row_norm[:, None]
    right_vec = start_raw / scale[:, None]
    left_prod = forward(start_raw)
    left_raw = left_prod / scale[:, None] - col_norm[:, None] * left_vec
    dir_now = right_vec
    solution = jnp.zeros_like(dir_now)
    phi_bar = row_norm
    diag_bar = col_norm
    for iteration in range(ITERATIONS):
        right_prod = backward(left_raw)
        row_norm = jnp.sqrt(all_sum(squares(left_raw), axes) + 1e-06)
        left_vec = left_raw / row_norm[:, None]
        right_raw = right_prod / row_norm[:, None] - row_norm[:, None] * right_vec
        if iteration + 1 < ITERATIONS:
            left_prod = forward(right_raw)
        col_norm = jnp.sqrt(all_sum(squares(right_raw), axes) + 1e-06)
        right_vec = right_raw / col_norm[:, None]
        if iteration + 1 < ITERATIONS:
            left_raw = left_prod / col_norm[:, None] - col_norm[:, None] * left_vec
        diag_new = jnp.sqrt(diag_bar * diag_bar + row_norm * row_norm)
        rot_cosine = diag_bar / diag_new
        rot_sine = row_norm / diag_new
        off_diag = rot_sine * col_norm
        diag_bar = -rot_cosine * col_norm
        phi_now = rot_cosine * phi_bar
        phi_bar = rot_sine * phi_bar
        solution = solution + (phi_now / diag_new)[:, None] * dir_now
        dir_now = right_vec - (off_diag / diag_new)[:, None] * dir_now
    return (solution, dir_now)


def solution(mesh):
    in_specs = (
        P("group", ("row", "col")),
        P(("group", "row", "col"), None, None, None),
        P(("group", "row", "col"), None),
        P(("group", "row", "col"), None),
        P(("group", "row", "col")),
    )
    out_specs = (P("group", ("row", "col")), P("group", ("row", "col")))
    return jax.shard_map(
        per_device, mesh=mesh, in_specs=in_specs, out_specs=out_specs, check_vma=False
    )
```

```python
import jax
import jax.numpy as jnp
from jax import lax
from jax.sharding import PartitionSpec as P
from jax.experimental import pallas as pl
from jax.experimental.pallas import tpu as pltpu

ROW_BLOCKS = 32
COL_BLOCKS = 64
ITERATIONS = 2


PRECISE = lax.Precision.HIGHEST
PRODUCT_PRECISION = lax.Precision.HIGH


def with_halo(shard, sides, width):
    for axis, dim in sides:
        peers, length = (lax.axis_size(axis), shard.shape[dim])
        up = [(i, (i + 1) % peers) for i in range(peers - 1)]
        down = [(j, i) for i, j in up]
        last = lax.slice_in_dim(shard, length - width, length, axis=dim)
        leading = lax.slice_in_dim(shard, 0, width, axis=dim)
        before = lax.ppermute(last, axis, up)
        after = lax.ppermute(leading, axis, down)
        shard = jnp.concatenate([before, shard, after], axis=dim)
    return shard


def from_behind(shard, axis, by):
    peers = lax.axis_size(axis)
    pairs = [(i, i + by) for i in range(peers) if 0 <= i + by < peers]
    return lax.ppermute(shard, axis, pairs)


def transpose_blocks(tile_stack, anchor):
    slots, edge, _ = tile_stack.shape
    step = 80 if slots % 80 == 0 else (32 if slots % 32 == 0 else 1)

    def body(anchor_ref, x_ref, o_ref):
        for i in range(step):
            o_ref[i] = x_ref[i].T

    nbytes = 2 * tile_stack.size * tile_stack.dtype.itemsize
    return pl.pallas_call(
        body,
        grid=(slots // step,),
        in_specs=[
            pl.BlockSpec(memory_space=pltpu.SMEM),
            pl.BlockSpec((step, edge, edge), lambda k: (k, 0, 0)),
        ],
        out_specs=pl.BlockSpec((step, edge, edge), lambda k: (k, 0, 0)),
        out_shape=jax.ShapeDtypeStruct(tile_stack.shape, tile_stack.dtype),
        cost_estimate=pl.CostEstimate(flops=0, transcendentals=0, bytes_accessed=nbytes),
    )(anchor, tile_stack)


def forward_local(window, tile_stack, rows_idx, cols_idx, live_slot):
    scenario_rows = window.shape[0]
    tile_edge = tile_stack.shape[1]
    pieces = window.reshape(scenario_rows, 3 * COL_BLOCKS, tile_edge)[:, cols_idx, :]
    products = (
        jnp.einsum("skj,kji->ksi", pieces, tile_stack, precision=PRODUCT_PRECISION)
    )
    onehot = (rows_idx[:, None] == jnp.arange(ROW_BLOCKS)[None, :]).astype(jnp.float32) * live_slot[:, None]
    summed = jnp.einsum("kr,ksi->sri", onehot, products, precision=PRODUCT_PRECISION)
    return summed.reshape(scenario_rows, ROW_BLOCKS * tile_edge)


def transpose_local(field, tile_stack, rows_idx, cols_idx, live_slot):
    scenario_rows = field.shape[0]
    tile_edge = tile_stack.shape[1]
    pieces = field.reshape(scenario_rows, ROW_BLOCKS, tile_edge)[:, rows_idx, :]
    products = (
        jnp.einsum("ski,kij->ksj", pieces, tile_stack, precision=PRODUCT_PRECISION)
    )
    onehot = (cols_idx[:, None] == jnp.arange(3 * COL_BLOCKS)[None, :]).astype(jnp.float32) * live_slot[:, None]
    summed = jnp.einsum("kc,ksj->scj", onehot, products, precision=PRODUCT_PRECISION)
    return summed.reshape(scenario_rows, 3 * COL_BLOCKS * tile_edge)


def forward_apply(vector, tile_stack, rows_idx, cols_idx, live_slot):
    window = with_halo(vector, ((("row", "col"), 1),), vector.shape[1])
    return forward_local(window, tile_stack, rows_idx, cols_idx, live_slot)


def transpose_apply(field, tile_stack, rows_idx, cols_idx, live_slot, beside=None):
    partial_sums = transpose_local(field, tile_stack, rows_idx, cols_idx, live_slot)
    band_width = partial_sums.shape[1] // 3
    lower = partial_sums[:, :band_width]
    middle = partial_sums[:, band_width : 2 * band_width]
    upper = partial_sums[:, 2 * band_width :]
    from_below = from_behind(upper, ("row", "col"), 1)
    from_above = from_behind(lower, ("row", "col"), -1)
    extra = None
    if beside is not None:
        extra = beside(middle[:1, :1])
        middle, extra = lax.optimization_barrier((middle, extra))
    result = middle + from_below + from_above
    return result, extra


def all_sum(values, axes):
    peers = 1
    for axis in axes:
        peers *= lax.axis_size(axis)
    spread = jnp.broadcast_to(values[None], (peers,) + values.shape)
    gathered = lax.all_to_all(spread, axes, 0, 0, tiled=True)
    return jnp.sum(gathered, axis=0)


def squares(field):
    return jnp.sum(field * field, axis=1)


def per_device(observed, blocks, block_rows, block_cols, counts):
    tile_stack = blocks[0]
    rows_idx = block_rows[0]
    cols_idx = block_cols[0]
    slot_ids = jnp.arange(tile_stack.shape[0])
    live_slot = (slot_ids < counts[0]).astype(jnp.float32)
    axes = ("row", "col")

    def backward(field):
        return transpose_apply(field, tile_stack, rows_idx, cols_idx, live_slot)[0]

    start_raw, tile_stack_t = transpose_apply(
        observed, tile_stack, rows_idx, cols_idx, live_slot,
        beside=lambda anchor: transpose_blocks(tile_stack, anchor),
    )

    def forward(vector):
        return forward_apply(vector, tile_stack_t, rows_idx, cols_idx, live_slot)

    totals = all_sum(jnp.stack([squares(observed), squares(start_raw)]), axes)
    row_norm = jnp.sqrt(totals[0] + 1e-06)
    col_norm = jnp.sqrt(totals[1] / (row_norm * row_norm) + 1e-06)
    scale = row_norm * col_norm
    left_vec = observed / row_norm[:, None]
    right_vec = start_raw / scale[:, None]
    left_prod = forward(start_raw)
    left_raw = left_prod / scale[:, None] - col_norm[:, None] * left_vec
    dir_now = right_vec
    solution = jnp.zeros_like(dir_now)
    phi_bar = row_norm
    diag_bar = col_norm
    for iteration in range(ITERATIONS):
        right_prod = backward(left_raw)
        row_norm = jnp.sqrt(all_sum(squares(left_raw), axes) + 1e-06)
        left_vec = left_raw / row_norm[:, None]
        right_raw = right_prod / row_norm[:, None] - row_norm[:, None] * right_vec
        if iteration + 1 < ITERATIONS:
            left_prod = forward(right_raw)
        col_norm = jnp.sqrt(all_sum(squares(right_raw), axes) + 1e-06)
        right_vec = right_raw / col_norm[:, None]
        if iteration + 1 < ITERATIONS:
            left_raw = left_prod / col_norm[:, None] - col_norm[:, None] * left_vec
        diag_new = jnp.sqrt(diag_bar * diag_bar + row_norm * row_norm)
        rot_cosine = diag_bar / diag_new
        rot_sine = row_norm / diag_new
        off_diag = rot_sine * col_norm
        diag_bar = -rot_cosine * col_norm
        phi_now = rot_cosine * phi_bar
        phi_bar = rot_sine * phi_bar
        solution = solution + (phi_now / diag_new)[:, None] * dir_now
        dir_now = right_vec - (off_diag / diag_new)[:, None] * dir_now
    return (solution, dir_now)


def solution(mesh):
    in_specs = (
        P("group", ("row", "col")),
        P(("group", "row", "col"), None, None, None),
        P(("group", "row", "col"), None),
        P(("group", "row", "col"), None),
        P(("group", "row", "col")),
    )
    out_specs = (P("group", ("row", "col")), P("group", ("row", "col")))
    return jax.shard_map(
        per_device, mesh=mesh, in_specs=in_specs, out_specs=out_specs, check_vma=False
    )
```

```python
import jax
import jax.numpy as jnp
from jax import lax
from jax.sharding import PartitionSpec as P
from jax.experimental import pallas as pl
from jax.experimental.pallas import tpu as pltpu

ROW_BLOCKS = 32
COL_BLOCKS = 64
ITERATIONS = 2


PRECISE = lax.Precision.HIGHEST
PRODUCT_PRECISION = lax.Precision.HIGH


def with_halo(shard, sides, width):
    for axis, dim in sides:
        peers, length = (lax.axis_size(axis), shard.shape[dim])
        up = [(i, (i + 1) % peers) for i in range(peers - 1)]
        down = [(j, i) for i, j in up]
        last = lax.slice_in_dim(shard, length - width, length, axis=dim)
        leading = lax.slice_in_dim(shard, 0, width, axis=dim)
        before = lax.ppermute(last, axis, up)
        after = lax.ppermute(leading, axis, down)
        shard = jnp.concatenate([before, shard, after], axis=dim)
    return shard


def from_behind(shard, axis, by):
    peers = lax.axis_size(axis)
    pairs = [(i, i + by) for i in range(peers) if 0 <= i + by < peers]
    return lax.ppermute(shard, axis, pairs)


def transpose_blocks(tile_stack, anchor):
    slots, edge, _ = tile_stack.shape
    step = 80 if slots % 80 == 0 else (32 if slots % 32 == 0 else 1)

    def body(anchor_ref, x_ref, o_ref):
        for i in range(step):
            o_ref[i] = x_ref[i].T

    nbytes = 2 * tile_stack.size * tile_stack.dtype.itemsize
    return pl.pallas_call(
        body,
        grid=(slots // step,),
        in_specs=[
            pl.BlockSpec(memory_space=pltpu.SMEM),
            pl.BlockSpec((step, edge, edge), lambda k: (k, 0, 0)),
        ],
        out_specs=pl.BlockSpec((step, edge, edge), lambda k: (k, 0, 0)),
        out_shape=jax.ShapeDtypeStruct(tile_stack.shape, tile_stack.dtype),
        cost_estimate=pl.CostEstimate(flops=0, transcendentals=0, bytes_accessed=nbytes),
    )(anchor, tile_stack)


def forward_local(window, tile_stack, rows_idx, cols_idx, live_slot):
    scenario_rows = window.shape[0]
    tile_edge = tile_stack.shape[1]
    pieces = window.reshape(scenario_rows, 3 * COL_BLOCKS, tile_edge)[:, cols_idx, :]
    products = (
        jnp.einsum("skj,kji->ksi", pieces, tile_stack, precision=PRODUCT_PRECISION) * live_slot[:, None, None]
    )
    onehot = (rows_idx[:, None] == jnp.arange(ROW_BLOCKS)[None, :]).astype(jnp.float32)
    summed = jnp.einsum("kr,ksi->sri", onehot, products, precision=PRODUCT_PRECISION)
    return summed.reshape(scenario_rows, ROW_BLOCKS * tile_edge)


def transpose_local(field, tile_stack, rows_idx, cols_idx, live_slot):
    scenario_rows = field.shape[0]
    tile_edge = tile_stack.shape[1]
    pieces = field.reshape(scenario_rows, ROW_BLOCKS, tile_edge)[:, rows_idx, :]
    products = (
        jnp.einsum("ski,kij->ksj", pieces, tile_stack, precision=PRODUCT_PRECISION) * live_slot[:, None, None]
    )
    bands = []
    for band in range(3):
        targets = band * COL_BLOCKS + jnp.arange(COL_BLOCKS)
        onehot = (cols_idx[:, None] == targets[None, :]).astype(jnp.float32)
        summed = jnp.einsum("kc,ksj->scj", onehot, products, precision=PRODUCT_PRECISION)
        bands.append(summed.reshape(scenario_rows, COL_BLOCKS * tile_edge))
    return bands


def forward_apply(vector, tile_stack, rows_idx, cols_idx, live_slot):
    window = with_halo(vector, ((("row", "col"), 1),), vector.shape[1])
    return forward_local(window, tile_stack, rows_idx, cols_idx, live_slot)


def transpose_apply(field, tile_stack, rows_idx, cols_idx, live_slot, beside=None):
    partial_sums = transpose_local(field, tile_stack, rows_idx, cols_idx, live_slot)
    lower, middle, upper = partial_sums
    from_below = from_behind(upper, ("row", "col"), 1)
    from_above = from_behind(lower, ("row", "col"), -1)
    extra = None
    if beside is not None:
        extra = beside(middle[:1, :1])
        middle, extra = lax.optimization_barrier((middle, extra))
    result = middle + from_below + from_above
    return result, extra


def all_sum(values, axes):
    peers = 1
    for axis in axes:
        peers *= lax.axis_size(axis)
    spread = jnp.broadcast_to(values[None], (peers,) + values.shape)
    gathered = lax.all_to_all(spread, axes, 0, 0, tiled=True)
    return jnp.sum(gathered, axis=0)


def squares(field):
    return jnp.sum(field * field, axis=1)


def per_device(observed, blocks, block_rows, block_cols, counts):
    tile_stack = blocks[0]
    rows_idx = block_rows[0]
    cols_idx = block_cols[0]
    slot_ids = jnp.arange(tile_stack.shape[0])
    live_slot = (slot_ids < counts[0]).astype(jnp.float32)
    axes = ("row", "col")

    def backward(field):
        return transpose_apply(field, tile_stack, rows_idx, cols_idx, live_slot)[0]

    start_raw, tile_stack_t = transpose_apply(
        observed, tile_stack, rows_idx, cols_idx, live_slot,
        beside=lambda anchor: transpose_blocks(tile_stack, anchor),
    )

    def forward(vector):
        return forward_apply(vector, tile_stack_t, rows_idx, cols_idx, live_slot)

    totals = all_sum(jnp.stack([squares(observed), squares(start_raw)]), axes)
    row_norm = jnp.sqrt(totals[0] + 1e-06)
    col_norm = jnp.sqrt(totals[1] / (row_norm * row_norm) + 1e-06)
    scale = row_norm * col_norm
    left_vec = observed / row_norm[:, None]
    right_vec = start_raw / scale[:, None]
    left_prod = forward(start_raw)
    left_raw = left_prod / scale[:, None] - col_norm[:, None] * left_vec
    dir_now = right_vec
    solution = jnp.zeros_like(dir_now)
    phi_bar = row_norm
    diag_bar = col_norm
    for iteration in range(ITERATIONS):
        right_prod = backward(left_raw)
        row_norm = jnp.sqrt(all_sum(squares(left_raw), axes) + 1e-06)
        left_vec = left_raw / row_norm[:, None]
        right_raw = right_prod / row_norm[:, None] - row_norm[:, None] * right_vec
        if iteration + 1 < ITERATIONS:
            left_prod = forward(right_raw)
        col_norm = jnp.sqrt(all_sum(squares(right_raw), axes) + 1e-06)
        right_vec = right_raw / col_norm[:, None]
        if iteration + 1 < ITERATIONS:
            left_raw = left_prod / col_norm[:, None] - col_norm[:, None] * left_vec
        diag_new = jnp.sqrt(diag_bar * diag_bar + row_norm * row_norm)
        rot_cosine = diag_bar / diag_new
        rot_sine = row_norm / diag_new
        off_diag = rot_sine * col_norm
        diag_bar = -rot_cosine * col_norm
        phi_now = rot_cosine * phi_bar
        phi_bar = rot_sine * phi_bar
        solution = solution + (phi_now / diag_new)[:, None] * dir_now
        dir_now = right_vec - (off_diag / diag_new)[:, None] * dir_now
    return (solution, dir_now)


def solution(mesh):
    in_specs = (
        P("group", ("row", "col")),
        P(("group", "row", "col"), None, None, None),
        P(("group", "row", "col"), None),
        P(("group", "row", "col"), None),
        P(("group", "row", "col")),
    )
    out_specs = (P("group", ("row", "col")), P("group", ("row", "col")))
    return jax.shard_map(
        per_device, mesh=mesh, in_specs=in_specs, out_specs=out_specs, check_vma=False
    )
```

```python
import jax
import jax.numpy as jnp
from jax import lax
from jax.sharding import PartitionSpec as P
from jax.experimental import pallas as pl
from jax.experimental.pallas import tpu as pltpu

ROW_BLOCKS = 32
COL_BLOCKS = 64
ITERATIONS = 2


PRECISE = lax.Precision.HIGHEST
PRODUCT_PRECISION = lax.Precision.HIGH


def with_halo(shard, sides, width):
    for axis, dim in sides:
        peers, length = (lax.axis_size(axis), shard.shape[dim])
        up = [(i, (i + 1) % peers) for i in range(peers - 1)]
        down = [(j, i) for i, j in up]
        last = lax.slice_in_dim(shard, length - width, length, axis=dim)
        leading = lax.slice_in_dim(shard, 0, width, axis=dim)
        before = lax.ppermute(last, axis, up)
        after = lax.ppermute(leading, axis, down)
        shard = jnp.concatenate([before, shard, after], axis=dim)
    return shard


def from_behind(shard, axis, by):
    peers = lax.axis_size(axis)
    pairs = [(i, i + by) for i in range(peers) if 0 <= i + by < peers]
    return lax.ppermute(shard, axis, pairs)


def transpose_blocks(tile_stack, anchor):
    slots, edge, _ = tile_stack.shape
    step = 80 if slots % 80 == 0 else (32 if slots % 32 == 0 else 1)

    def body(anchor_ref, x_ref, o_ref):
        for i in range(step):
            o_ref[i] = x_ref[i].T

    nbytes = 2 * tile_stack.size * tile_stack.dtype.itemsize
    return pl.pallas_call(
        body,
        grid=(slots // step,),
        in_specs=[
            pl.BlockSpec(memory_space=pltpu.SMEM),
            pl.BlockSpec((step, edge, edge), lambda k: (k, 0, 0)),
        ],
        out_specs=pl.BlockSpec((step, edge, edge), lambda k: (k, 0, 0)),
        out_shape=jax.ShapeDtypeStruct(tile_stack.shape, tile_stack.dtype),
        cost_estimate=pl.CostEstimate(flops=0, transcendentals=0, bytes_accessed=nbytes),
    )(anchor, tile_stack)


def forward_local(window, tile_stack, rows_idx, cols_idx, live_slot):
    scenario_rows = window.shape[0]
    tile_edge = tile_stack.shape[1]
    pieces = window.reshape(scenario_rows, 3 * COL_BLOCKS, tile_edge)[:, cols_idx, :]
    products = (
        jnp.einsum("skj,kji->ksi", pieces, tile_stack, precision=PRODUCT_PRECISION) * live_slot[:, None, None]
    )
    onehot = (rows_idx[:, None] == jnp.arange(ROW_BLOCKS)[None, :]).astype(jnp.float32)
    summed = jnp.einsum("kr,ksi->sri", onehot, products, precision=PRODUCT_PRECISION)
    return summed.reshape(scenario_rows, ROW_BLOCKS * tile_edge)


def transpose_local(field, tile_stack, rows_idx, cols_idx, live_slot):
    scenario_rows = field.shape[0]
    tile_edge = tile_stack.shape[1]
    pieces = field.reshape(scenario_rows, ROW_BLOCKS, tile_edge)[:, rows_idx, :]
    products = (
        jnp.einsum("ski,kij->ksj", pieces, tile_stack, precision=PRODUCT_PRECISION) * live_slot[:, None, None]
    )
    onehot = (cols_idx[:, None] == jnp.arange(3 * COL_BLOCKS)[None, :]).astype(jnp.float32)
    summed = jnp.einsum("kc,ksj->scj", onehot, products, precision=PRODUCT_PRECISION)
    return summed.reshape(scenario_rows, 3 * COL_BLOCKS * tile_edge)


def forward_apply(vector, tile_stack, rows_idx, cols_idx, live_slot):
    window = with_halo(vector, ((("row", "col"), 1),), vector.shape[1])
    return forward_local(window, tile_stack, rows_idx, cols_idx, live_slot)


def transpose_apply(field, tile_stack, rows_idx, cols_idx, live_slot, beside=None):
    partial_sums = transpose_local(field, tile_stack, rows_idx, cols_idx, live_slot)
    band_width = partial_sums.shape[1] // 3
    lower = partial_sums[:, :band_width]
    middle = partial_sums[:, band_width : 2 * band_width]
    upper = partial_sums[:, 2 * band_width :]
    from_below = from_behind(upper, ("row", "col"), 1)
    from_above = from_behind(lower, ("row", "col"), -1)
    extra = None
    if beside is not None:
        extra = beside(middle[:1, :1])
        middle, extra = lax.optimization_barrier((middle, extra))
    result = middle + from_below + from_above
    return result, extra


def all_sum(values, axes):
    peers = 1
    for axis in axes:
        peers *= lax.axis_size(axis)
    spread = jnp.broadcast_to(values[None], (peers,) + values.shape)
    gathered = lax.all_to_all(spread, axes, 0, 0, tiled=True)
    return jnp.sum(gathered, axis=0)


def squares(field):
    return jnp.sum(field * field, axis=1)


def per_device(observed, blocks, block_rows, block_cols, counts):
    tile_stack = blocks[0]
    rows_idx = block_rows[0]
    cols_idx = block_cols[0]
    slot_ids = jnp.arange(tile_stack.shape[0])
    live_slot = (slot_ids < counts[0]).astype(jnp.float32)
    axes = ("row", "col")

    def backward(field):
        return transpose_apply(field, tile_stack, rows_idx, cols_idx, live_slot)[0]

    start_raw, tile_stack_t = transpose_apply(
        observed, tile_stack, rows_idx, cols_idx, live_slot,
        beside=lambda anchor: transpose_blocks(tile_stack, anchor),
    )

    def forward(vector):
        return forward_apply(vector, tile_stack_t, rows_idx, cols_idx, live_slot)

    totals = all_sum(jnp.stack([squares(observed), squares(start_raw)]), axes)
    start_raw, totals = lax.optimization_barrier((start_raw, totals))
    row_norm = jnp.sqrt(totals[0] + 1e-06)
    col_norm = jnp.sqrt(totals[1] / (row_norm * row_norm) + 1e-06)
    scale = row_norm * col_norm
    left_vec = observed / row_norm[:, None]
    right_vec = start_raw / scale[:, None]
    left_prod = forward(start_raw)
    left_raw = left_prod / scale[:, None] - col_norm[:, None] * left_vec
    dir_now = right_vec
    solution = jnp.zeros_like(dir_now)
    phi_bar = row_norm
    diag_bar = col_norm
    for iteration in range(ITERATIONS):
        right_prod = backward(left_raw)
        row_norm = jnp.sqrt(all_sum(squares(left_raw), axes) + 1e-06)
        left_vec = left_raw / row_norm[:, None]
        right_raw = right_prod / row_norm[:, None] - row_norm[:, None] * right_vec
        if iteration + 1 < ITERATIONS:
            left_prod = forward(right_raw)
        col_norm = jnp.sqrt(all_sum(squares(right_raw), axes) + 1e-06)
        right_vec = right_raw / col_norm[:, None]
        if iteration + 1 < ITERATIONS:
            left_raw = left_prod / col_norm[:, None] - col_norm[:, None] * left_vec
        diag_new = jnp.sqrt(diag_bar * diag_bar + row_norm * row_norm)
        rot_cosine = diag_bar / diag_new
        rot_sine = row_norm / diag_new
        off_diag = rot_sine * col_norm
        diag_bar = -rot_cosine * col_norm
        phi_now = rot_cosine * phi_bar
        phi_bar = rot_sine * phi_bar
        solution = solution + (phi_now / diag_new)[:, None] * dir_now
        dir_now = right_vec - (off_diag / diag_new)[:, None] * dir_now
    return (solution, dir_now)


def solution(mesh):
    in_specs = (
        P("group", ("row", "col")),
        P(("group", "row", "col"), None, None, None),
        P(("group", "row", "col"), None),
        P(("group", "row", "col"), None),
        P(("group", "row", "col")),
    )
    out_specs = (P("group", ("row", "col")), P("group", ("row", "col")))
    return jax.shard_map(
        per_device, mesh=mesh, in_specs=in_specs, out_specs=out_specs, check_vma=False
    )
```

```python
import jax
import jax.numpy as jnp
from jax import lax
from jax.sharding import PartitionSpec as P
from jax.experimental import pallas as pl
from jax.experimental.pallas import tpu as pltpu

ROW_BLOCKS = 32
COL_BLOCKS = 64
ITERATIONS = 2


PRECISE = lax.Precision.HIGHEST
PRODUCT_PRECISION = lax.Precision.HIGH


def with_halo(shard, sides, width):
    for axis, dim in sides:
        peers, length = (lax.axis_size(axis), shard.shape[dim])
        up = [(i, (i + 1) % peers) for i in range(peers - 1)]
        down = [(j, i) for i, j in up]
        last = lax.slice_in_dim(shard, length - width, length, axis=dim)
        leading = lax.slice_in_dim(shard, 0, width, axis=dim)
        before = lax.ppermute(last, axis, up)
        after = lax.ppermute(leading, axis, down)
        shard = jnp.concatenate([before, shard, after], axis=dim)
    return shard


def from_behind(shard, axis, by):
    peers = lax.axis_size(axis)
    pairs = [(i, i + by) for i in range(peers) if 0 <= i + by < peers]
    return lax.ppermute(shard, axis, pairs)


def transpose_blocks(tile_stack, anchor, first, count, into=None):
    slots, edge, _ = tile_stack.shape
    step = count if first % count == 0 else 1
    offset = first // step

    def body(anchor_ref, x_ref, *refs):
        o_ref = refs[-1]
        for i in range(step):
            o_ref[i] = x_ref[i].T

    in_specs = [
        pl.BlockSpec(memory_space=pltpu.SMEM),
        pl.BlockSpec((step, edge, edge), lambda k: (k + offset, 0, 0)),
    ]
    operands = [anchor, tile_stack]
    aliases = {}
    if into is not None:
        in_specs.append(pl.BlockSpec(memory_space=pl.ANY))
        operands.append(into)
        aliases = {2: 0}
    nbytes = 2 * count * edge * edge * tile_stack.dtype.itemsize
    return pl.pallas_call(
        body,
        grid=(count // step,),
        in_specs=in_specs,
        out_specs=pl.BlockSpec((step, edge, edge), lambda k: (k + offset, 0, 0)),
        out_shape=jax.ShapeDtypeStruct(tile_stack.shape, tile_stack.dtype),
        input_output_aliases=aliases,
        cost_estimate=pl.CostEstimate(flops=0, transcendentals=0, bytes_accessed=nbytes),
    )(*operands)


def forward_local(window, tile_stack, rows_idx, cols_idx, live_slot):
    scenario_rows = window.shape[0]
    tile_edge = tile_stack.shape[1]
    pieces = window.reshape(scenario_rows, 3 * COL_BLOCKS, tile_edge)[:, cols_idx, :]
    products = (
        jnp.einsum("skj,kji->ksi", pieces, tile_stack, precision=PRODUCT_PRECISION) * live_slot[:, None, None]
    )
    onehot = (rows_idx[:, None] == jnp.arange(ROW_BLOCKS)[None, :]).astype(jnp.float32)
    summed = jnp.einsum("kr,ksi->sri", onehot, products, precision=PRODUCT_PRECISION)
    return summed.reshape(scenario_rows, ROW_BLOCKS * tile_edge)


def transpose_local(field, tile_stack, rows_idx, cols_idx, live_slot):
    scenario_rows = field.shape[0]
    tile_edge = tile_stack.shape[1]
    pieces = field.reshape(scenario_rows, ROW_BLOCKS, tile_edge)[:, rows_idx, :]
    products = (
        jnp.einsum("ski,kij->ksj", pieces, tile_stack, precision=PRODUCT_PRECISION) * live_slot[:, None, None]
    )
    onehot = (cols_idx[:, None] == jnp.arange(3 * COL_BLOCKS)[None, :]).astype(jnp.float32)
    summed = jnp.einsum("kc,ksj->scj", onehot, products, precision=PRODUCT_PRECISION)
    return summed.reshape(scenario_rows, 3 * COL_BLOCKS * tile_edge)


def forward_apply(vector, tile_stack, rows_idx, cols_idx, live_slot):
    window = with_halo(vector, ((("row", "col"), 1),), vector.shape[1])
    return forward_local(window, tile_stack, rows_idx, cols_idx, live_slot)


def transpose_apply(field, tile_stack, rows_idx, cols_idx, live_slot, beside=None):
    partial_sums = transpose_local(field, tile_stack, rows_idx, cols_idx, live_slot)
    band_width = partial_sums.shape[1] // 3
    lower = partial_sums[:, :band_width]
    middle = partial_sums[:, band_width : 2 * band_width]
    upper = partial_sums[:, 2 * band_width :]
    from_below = from_behind(upper, ("row", "col"), 1)
    from_above = from_behind(lower, ("row", "col"), -1)
    extra = None
    if beside is not None:
        extra = beside(middle[:1, :1])
        middle, extra = lax.optimization_barrier((middle, extra))
    result = middle + from_below + from_above
    return result, extra


def all_sum(values, axes):
    peers = 1
    for axis in axes:
        peers *= lax.axis_size(axis)
    spread = jnp.broadcast_to(values[None], (peers,) + values.shape)
    gathered = lax.all_to_all(spread, axes, 0, 0, tiled=True)
    return jnp.sum(gathered, axis=0)


def squares(field):
    return jnp.sum(field * field, axis=1)


def per_device(observed, blocks, block_rows, block_cols, counts):
    tile_stack = blocks[0]
    rows_idx = block_rows[0]
    cols_idx = block_cols[0]
    slot_ids = jnp.arange(tile_stack.shape[0])
    live_slot = (slot_ids < counts[0]).astype(jnp.float32)
    axes = ("row", "col")

    def backward(field):
        return transpose_apply(field, tile_stack, rows_idx, cols_idx, live_slot)[0]

    slots = tile_stack.shape[0]
    half = slots // 2
    start_raw, first_half = transpose_apply(
        observed, tile_stack, rows_idx, cols_idx, live_slot,
        beside=lambda anchor: transpose_blocks(tile_stack, anchor, 0, half),
    )
    tile_stack_t = transpose_blocks(tile_stack, start_raw[:1, :1], half, slots - half, into=first_half)

    def forward(vector):
        return forward_apply(vector, tile_stack_t, rows_idx, cols_idx, live_slot)

    totals = all_sum(jnp.stack([squares(observed), squares(start_raw)]), axes)
    row_norm = jnp.sqrt(totals[0] + 1e-06)
    col_norm = jnp.sqrt(totals[1] / (row_norm * row_norm) + 1e-06)
    scale = row_norm * col_norm
    left_vec = observed / row_norm[:, None]
    right_vec = start_raw / scale[:, None]
    left_prod = forward(start_raw)
    left_raw = left_prod / scale[:, None] - col_norm[:, None] * left_vec
    dir_now = right_vec
    solution = jnp.zeros_like(dir_now)
    phi_bar = row_norm
    diag_bar = col_norm
    for iteration in range(ITERATIONS):
        right_prod = backward(left_raw)
        row_norm = jnp.sqrt(all_sum(squares(left_raw), axes) + 1e-06)
        left_vec = left_raw / row_norm[:, None]
        right_raw = right_prod / row_norm[:, None] - row_norm[:, None] * right_vec
        if iteration + 1 < ITERATIONS:
            left_prod = forward(right_raw)
        col_norm = jnp.sqrt(all_sum(squares(right_raw), axes) + 1e-06)
        right_vec = right_raw / col_norm[:, None]
        if iteration + 1 < ITERATIONS:
            left_raw = left_prod / col_norm[:, None] - col_norm[:, None] * left_vec
        diag_new = jnp.sqrt(diag_bar * diag_bar + row_norm * row_norm)
        rot_cosine = diag_bar / diag_new
        rot_sine = row_norm / diag_new
        off_diag = rot_sine * col_norm
        diag_bar = -rot_cosine * col_norm
        phi_now = rot_cosine * phi_bar
        phi_bar = rot_sine * phi_bar
        solution = solution + (phi_now / diag_new)[:, None] * dir_now
        dir_now = right_vec - (off_diag / diag_new)[:, None] * dir_now
    return (solution, dir_now)


def solution(mesh):
    in_specs = (
        P("group", ("row", "col")),
        P(("group", "row", "col"), None, None, None),
        P(("group", "row", "col"), None),
        P(("group", "row", "col"), None),
        P(("group", "row", "col")),
    )
    out_specs = (P("group", ("row", "col")), P("group", ("row", "col")))
    return jax.shard_map(
        per_device, mesh=mesh, in_specs=in_specs, out_specs=out_specs, check_vma=False
    )
```

```python
import jax
import jax.numpy as jnp
from jax import lax
from jax.sharding import PartitionSpec as P
from jax.experimental import pallas as pl
from jax.experimental.pallas import tpu as pltpu

ROW_BLOCKS = 32
COL_BLOCKS = 64
ITERATIONS = 2


PRECISE = lax.Precision.HIGHEST
PRODUCT_PRECISION = lax.Precision.HIGH


def with_halo(shard, sides, width):
    for axis, dim in sides:
        peers, length = (lax.axis_size(axis), shard.shape[dim])
        up = [(i, (i + 1) % peers) for i in range(peers - 1)]
        down = [(j, i) for i, j in up]
        last = lax.slice_in_dim(shard, length - width, length, axis=dim)
        leading = lax.slice_in_dim(shard, 0, width, axis=dim)
        before = lax.ppermute(last, axis, up)
        after = lax.ppermute(leading, axis, down)
        shard = jnp.concatenate([before, shard, after], axis=dim)
    return shard


def from_behind(shard, axis, by):
    peers = lax.axis_size(axis)
    pairs = [(i, i + by) for i in range(peers) if 0 <= i + by < peers]
    return lax.ppermute(shard, axis, pairs)


def transpose_blocks(tile_stack, anchor):
    slots, edge, _ = tile_stack.shape
    step = 80 if slots % 80 == 0 else (32 if slots % 32 == 0 else 1)

    def body(anchor_ref, x_ref, o_ref):
        for i in range(step):
            o_ref[i] = x_ref[i].T

    nbytes = 2 * tile_stack.size * tile_stack.dtype.itemsize
    return pl.pallas_call(
        body,
        grid=(slots // step,),
        in_specs=[
            pl.BlockSpec(memory_space=pltpu.SMEM),
            pl.BlockSpec((step, edge, edge), lambda k: (k, 0, 0)),
        ],
        out_specs=pl.BlockSpec((step, edge, edge), lambda k: (k, 0, 0)),
        out_shape=jax.ShapeDtypeStruct(tile_stack.shape, tile_stack.dtype),
        cost_estimate=pl.CostEstimate(flops=0, transcendentals=0, bytes_accessed=nbytes),
    )(anchor, tile_stack)


def forward_local(window, tile_stack, rows_idx, cols_idx, live_slot):
    scenario_rows = window.shape[0]
    tile_edge = tile_stack.shape[1]
    pieces = window.reshape(scenario_rows, 3 * COL_BLOCKS, tile_edge)[:, cols_idx, :]
    products = (
        jnp.einsum("skj,kji->ksi", pieces, tile_stack, precision=PRODUCT_PRECISION) * live_slot[:, None, None]
    )
    onehot = (rows_idx[:, None] == jnp.arange(ROW_BLOCKS)[None, :]).astype(jnp.float32)
    summed = jnp.einsum("kr,ksi->sri", onehot, products, precision=PRODUCT_PRECISION)
    return summed.reshape(scenario_rows, ROW_BLOCKS * tile_edge)


def transpose_local(field, tile_stack, rows_idx, cols_idx, live_slot):
    scenario_rows = field.shape[0]
    tile_edge = tile_stack.shape[1]
    pieces = field.reshape(scenario_rows, ROW_BLOCKS, tile_edge)[:, rows_idx, :]
    products = (
        jnp.einsum("ski,kij->ksj", pieces, tile_stack, precision=PRODUCT_PRECISION) * live_slot[:, None, None]
    )
    onehot = (cols_idx[:, None] == jnp.arange(3 * COL_BLOCKS)[None, :]).astype(jnp.float32)
    summed = jnp.einsum("kc,ksj->scj", onehot, products, precision=PRODUCT_PRECISION)
    return summed.reshape(scenario_rows, 3 * COL_BLOCKS * tile_edge)


def forward_apply(vector, tile_stack, rows_idx, cols_idx, live_slot):
    window = with_halo(vector, ((("row", "col"), 1),), vector.shape[1])
    return forward_local(window, tile_stack, rows_idx, cols_idx, live_slot)


def transpose_apply(field, tile_stack, rows_idx, cols_idx, live_slot, beside=None):
    partial_sums = transpose_local(field, tile_stack, rows_idx, cols_idx, live_slot)
    band_width = partial_sums.shape[1] // 3
    lower = partial_sums[:, :band_width]
    middle = partial_sums[:, band_width : 2 * band_width]
    upper = partial_sums[:, 2 * band_width :]
    from_below = from_behind(upper, ("row", "col"), 1)
    from_above = from_behind(lower, ("row", "col"), -1)
    extra = None
    if beside is not None:
        extra = beside(middle[:1, :1])
        middle, extra = lax.optimization_barrier((middle, extra))
    result = middle + from_below + from_above
    return result, extra


def all_sum(values, axes):
    peers = 1
    for axis in axes:
        peers *= lax.axis_size(axis)
    spread = jnp.broadcast_to(values[None], (peers,) + values.shape)
    gathered = lax.all_to_all(spread, axes, 0, 0, tiled=True)
    return jnp.sum(gathered, axis=0)


def xor_sum(values, axes):
    peers = 1
    for axis in axes:
        peers *= lax.axis_size(axis)
    if peers & (peers - 1):
        return all_sum(values, axes)
    shift = 1
    while shift < peers:
        width = 4 if shift * 4 <= peers else 2
        parts = [values] + [
            lax.ppermute(values, axes, [(i, i ^ (k * shift)) for i in range(peers)])
            for k in range(1, width)
        ]
        values = (parts[0] + parts[1]) + (parts[2] + parts[3]) if width == 4 else parts[0] + parts[1]
        shift *= width
    return values


def squares(field):
    return jnp.sum(field * field, axis=1)


def per_device(observed, blocks, block_rows, block_cols, counts):
    tile_stack = blocks[0]
    rows_idx = block_rows[0]
    cols_idx = block_cols[0]
    slot_ids = jnp.arange(tile_stack.shape[0])
    live_slot = (slot_ids < counts[0]).astype(jnp.float32)
    axes = ("row", "col")

    def backward(field):
        return transpose_apply(field, tile_stack, rows_idx, cols_idx, live_slot)[0]

    start_raw, tile_stack_t = transpose_apply(
        observed, tile_stack, rows_idx, cols_idx, live_slot,
        beside=lambda anchor: transpose_blocks(tile_stack, anchor),
    )

    def forward(vector):
        return forward_apply(vector, tile_stack_t, rows_idx, cols_idx, live_slot)

    totals = all_sum(jnp.stack([squares(observed), squares(start_raw)]), axes)
    row_norm = jnp.sqrt(totals[0] + 1e-06)
    col_norm = jnp.sqrt(totals[1] / (row_norm * row_norm) + 1e-06)
    scale = row_norm * col_norm
    left_vec = observed / row_norm[:, None]
    right_vec = start_raw / scale[:, None]
    left_prod = forward(start_raw)
    left_raw = left_prod / scale[:, None] - col_norm[:, None] * left_vec
    dir_now = right_vec
    solution = jnp.zeros_like(dir_now)
    phi_bar = row_norm
    diag_bar = col_norm
    for iteration in range(ITERATIONS):
        right_prod = backward(left_raw)
        row_norm = jnp.sqrt(all_sum(squares(left_raw), axes) + 1e-06)
        left_vec = left_raw / row_norm[:, None]
        right_raw = right_prod / row_norm[:, None] - row_norm[:, None] * right_vec
        if iteration + 1 < ITERATIONS:
            left_prod = forward(right_raw)
        reduce = all_sum if iteration + 1 < ITERATIONS else xor_sum
        col_norm = jnp.sqrt(reduce(squares(right_raw), axes) + 1e-06)
        right_vec = right_raw / col_norm[:, None]
        if iteration + 1 < ITERATIONS:
            left_raw = left_prod / col_norm[:, None] - col_norm[:, None] * left_vec
        diag_new = jnp.sqrt(diag_bar * diag_bar + row_norm * row_norm)
        rot_cosine = diag_bar / diag_new
        rot_sine = row_norm / diag_new
        off_diag = rot_sine * col_norm
        diag_bar = -rot_cosine * col_norm
        phi_now = rot_cosine * phi_bar
        phi_bar = rot_sine * phi_bar
        solution = solution + (phi_now / diag_new)[:, None] * dir_now
        dir_now = right_vec - (off_diag / diag_new)[:, None] * dir_now
    return (solution, dir_now)


def solution(mesh):
    in_specs = (
        P("group", ("row", "col")),
        P(("group", "row", "col"), None, None, None),
        P(("group", "row", "col"), None),
        P(("group", "row", "col"), None),
        P(("group", "row", "col")),
    )
    out_specs = (P("group", ("row", "col")), P("group", ("row", "col")))
    return jax.shard_map(
        per_device, mesh=mesh, in_specs=in_specs, out_specs=out_specs, check_vma=False
    )
```
